32 devices in a mesh: groups: 2 (over y), video: 8 (over z, x), fsdp: 2 (over core).
Axes of the slice: x: 2, y: 2, z: 4, core: 2. Of those that a mesh axis runs over, the one named last changes fastest.
Arguments:
- video: bfloat16 [32, 32, 16, 512], P(('groups', 'video', 'fsdp')), parts along dimension 0, may hold values from -6 to 6
- w_spatial: bfloat16 [3, 3, 512, 512], P(None, None, 'fsdp'), may hold values from -0.09375 to 0.09375
- norm_gain: float32 [512], replicated, may hold values from 0.1 to 1.9
- norm_shift: float32 [512], replicated, may hold values from -3 to 3
- w_time: bfloat16 [3, 512, 512], P(None, 'fsdp'), may hold values from -0.15625 to 0.15625
Outputs:
- result: bfloat16 [32, 32, 16, 512], P(('groups', 'video', 'fsdp')), parts along dimension 0
The draws below stay inside these ranges and needn't reach their ends.
There are 2 independent parts, one for each index of `groups`. The reference program is written for one: setup_inputs(seed, part) draws one part's arguments, and reference() takes and returns one part's arrays. A program takes and returns all parts, laid end to end along the dimension named above; an argument that names none is the same for every part. Nothing has to cross between parts.
All inputs are finite; a program needn't handle non-finite values.
Results may differ from the reference program's by a relative error of at most 0.0049.
Values may be sent and summed in bfloat16 or wider, within the bound.
No kernel may reach another device: no remote copies, remote signals or barrier semaphores. Data moves between devices by JAX's collectives and lax.ppermute only.
A program may use at most 64 MiB of HBM per device.

```python
import jax
import jax.numpy as jnp
from jax import lax

CHANNELS = 512
GROUPS = 32
CLIP = 16
HEIGHT = 32
WIDTH = 16
FRAMES = 16


def level_of(own_key, dims, split, low, top_value):
    def one(dim, shards_of):
        heights = jax.random.uniform(jax.random.fold_in(jax.random.fold_in(own_key, 6), dim), (shards_of,), jnp.float32, low / len(split), top_value / len(split))
        return jnp.repeat(jnp.exp(heights), dims[dim] // shards_of).reshape((-1,) + (1,) * (len(dims) - dim - 1))

    factor_of = one(*split[0])
    for cut in split[1:]:
        factor_of = factor_of * one(*cut)
    return factor_of


def noise(own_key, dims, deviation, most, split=(), dtype=jnp.bfloat16):
    drawn = deviation * jax.random.normal(own_key, dims, jnp.float32)
    if split:
        drawn = drawn * level_of(own_key, dims, split, -0.22, 0.18)
    return jnp.clip(drawn, -most, most).astype(dtype)


def setup_inputs(seed: int = 0, part: int = 0) -> dict:
    seeds = jax.random.split(jax.random.key(seed), 6)
    part_keys = jax.random.split(jax.random.fold_in(seeds[5], part), 6)
    video = noise(part_keys[0], (FRAMES, HEIGHT, WIDTH, CHANNELS), 1.0, 6.0, ((0, 16),))
    w_spatial = noise(seeds[1], (3, 3, CHANNELS, CHANNELS), (9 * CHANNELS) ** -0.5, 0.09375, ((2, 2),))
    norm_gain = jnp.clip(1.0 + 0.18 * jax.random.normal(seeds[2], (CHANNELS,), jnp.float32), 0.1, 1.9)
    norm_shift = noise(seeds[3], (CHANNELS,), 0.5, 3.0, (), jnp.float32)
    w_time = noise(seeds[4], (3, CHANNELS, CHANNELS), (3 * CHANNELS) ** -0.5, 0.15625, ((1, 2),))
    return {"video": video, "w_spatial": w_spatial, "norm_gain": norm_gain, "norm_shift": norm_shift, "w_time": w_time}


def reference(video, w_spatial, norm_gain, norm_shift, w_time):
    count, height, width, channels = video.shape
    spatial = lax.conv_general_dilated(video, w_spatial, (1, 1), ((1, 1), (1, 1)), dimension_numbers=('NHWC', 'HWIO', 'NHWC'), preferred_element_type=jnp.float32)
    grouped = spatial.reshape(count, height * width, GROUPS, channels // GROUPS)
    mean = lax.optimization_barrier(jnp.mean(grouped, axis=(1, 3), keepdims=True))
    variance = lax.optimization_barrier(jnp.mean(jnp.square(grouped - mean), axis=(1, 3), keepdims=True))
    normed = ((grouped - mean) * lax.rsqrt(variance + 1e-05)).reshape(count, height * width, channels)
    hidden = jax.nn.silu(normed * norm_gain + norm_shift).astype(jnp.bfloat16)
    clips = hidden.reshape(count // CLIP, CLIP, height * width, channels)
    padded = jnp.pad(clips, ((0, 0), (1, 1), (0, 0), (0, 0)))
    total = jnp.zeros((count * height * width, channels), jnp.float32)
    for tap in range(3):
        shifted = padded[:, tap:tap + CLIP].reshape(-1, channels)
        total = total + jnp.dot(shifted, w_time[tap], preferred_element_type=jnp.float32)
    result = hidden.reshape(-1, channels).astype(jnp.float32) + total
    return result.astype(jnp.bfloat16).reshape(count, height, width, channels)
```

```python
import jax
import jax.numpy as jnp
from jax import lax
from jax.sharding import PartitionSpec as P

GROUPS = 32
CLIP = 16


def swap_pair(block):
    return lax.ppermute(block, "fsdp", [(0, 1), (1, 0)])


def shift_frames(block, step):
    count = lax.axis_size("video") * lax.axis_size("fsdp")
    route = [(j, j + step) for j in range(count) if 0 <= j + step < count]
    return lax.ppermute(block, ("video", "fsdp"), route)


def channel_half(block, side, span):
    return lax.dynamic_slice_in_dim(block, side * span, span, axis=block.ndim - 1)


def spatial_conv(frames, w_spatial):
    side = lax.axis_index("fsdp")
    span = w_spatial.shape[2]
    other_weight = swap_pair(w_spatial)
    numbers = ("NHWC", "HWIO", "NHWC")
    mine = lax.conv_general_dilated(
        channel_half(frames, side, span), w_spatial, (1, 1), ((1, 1), (1, 1)),
        dimension_numbers=numbers, preferred_element_type=jnp.float32,
    )
    other = lax.conv_general_dilated(
        channel_half(frames, 1 - side, span), other_weight, (1, 1), ((1, 1), (1, 1)),
        dimension_numbers=numbers, preferred_element_type=jnp.float32,
    )
    return mine + other


def body(video, w_spatial, norm_gain, norm_shift, w_time):
    count, height, width, channels = video.shape
    other_time = swap_pair(w_time)
    spatial = spatial_conv(video, w_spatial)
    grouped = spatial.reshape(count, height * width, GROUPS, channels // GROUPS)
    mean = jnp.mean(grouped, axis=(1, 3), keepdims=True)
    variance = jnp.mean(jnp.square(grouped - mean), axis=(1, 3), keepdims=True)
    normed = ((grouped - mean) * lax.rsqrt(variance + 1e-05)).reshape(
        count, height * width, channels
    )
    hidden = jax.nn.silu(normed * norm_gain + norm_shift).astype(jnp.bfloat16)

    from_before = shift_frames(hidden[count - 1 :], 1)
    from_after = shift_frames(hidden[:1], -1)
    previous = jnp.concatenate([from_before, hidden[:-1]], axis=0)
    following = jnp.concatenate([hidden[1:], from_after], axis=0)
    position = lax.axis_index("video") * lax.axis_size("fsdp") + lax.axis_index("fsdp")
    frame_ids = position * count + jnp.arange(count)
    keep_before = (frame_ids % CLIP != 0)[:, None, None]
    keep_after = (frame_ids % CLIP != CLIP - 1)[:, None, None]
    previous = jnp.where(keep_before, previous, jnp.zeros_like(previous))
    following = jnp.where(keep_after, following, jnp.zeros_like(following))

    side = lax.axis_index("fsdp")
    span = w_time.shape[1]
    rows = count * height * width
    total = jnp.zeros((rows, channels), jnp.float32)
    for tap, frames in enumerate((previous, hidden, following)):
        flat = frames.reshape(rows, channels)
        total = total + jnp.dot(
            channel_half(flat, side, span), w_time[tap], preferred_element_type=jnp.float32
        )
        total = total + jnp.dot(
            channel_half(flat, 1 - side, span), other_time[tap], preferred_element_type=jnp.float32
        )
    mixed = (hidden.reshape(rows, channels).astype(jnp.float32) + total).astype(jnp.bfloat16)
    return mixed.reshape(count, height, width, channels)


def solution(mesh):
    placed = (
        P(("groups", "video", "fsdp"), None, None, None),
        P(None, None, "fsdp", None),
        P(),
        P(),
        P(None, "fsdp", None),
    )
    return jax.shard_map(
        body,
        mesh=mesh,
        in_specs=placed,
        out_specs=P(("groups", "video", "fsdp"), None, None, None),
        check_vma=False,
    )
```

```python
import functools

import jax
import jax.numpy as jnp
from jax import lax
from jax.experimental import pallas as pl
from jax.experimental.pallas import tpu as pltpu
from jax.sharding import PartitionSpec as P

GROUPS = 32
CLIP = 16
EPS = 1e-05


def swap_pair(block):
    return lax.ppermute(block, "fsdp", [(0, 1), (1, 0)])


def group_sum(row, size):
    lanes = lax.broadcasted_iota(jnp.int32, row.shape, 1)
    width = row.shape[1]
    step = 1
    while step < size:
        up = pltpu.roll(row, width - step, 1)
        down = pltpu.roll(row, step, 1)
        row = row + jnp.where((lanes & step) == 0, up, down)
        step *= 2
    return row


def conv_norm_kernel(side_ref, xa_ref, xb_ref, wa_ref, wb_ref, gain_ref, shift_ref, o_ref,
                     xs_ref, acc_ref, *, width, group):
    tap = pl.program_id(0)
    rows, half = xa_ref.shape

    @pl.when(tap == 0)
    def _prepare():
        col = lax.broadcasted_iota(jnp.int32, (rows, half), 0) % width
        zeros = jnp.zeros((width, half), jnp.bfloat16)
        for h, x_ref in enumerate((xa_ref, xb_ref)):
            xf = x_ref[...].astype(jnp.float32)
            left = jnp.where(col == 0, 0.0, pltpu.roll(xf, 1, 0))
            right = jnp.where(col == width - 1, 0.0, pltpu.roll(xf, rows - 1, 0))
            for dx, v in enumerate((left, xf, right)):
                xs_ref[h, dx, :width, :] = zeros
                xs_ref[h, dx, width : width + rows, :] = v.astype(jnp.bfloat16)
                xs_ref[h, dx, width + rows :, :] = zeros
        acc_ref[...] = jnp.zeros_like(acc_ref)

    dy = tap // 3
    dx = tap % 3
    start = pl.multiple_of(dy * width, width)
    a = xs_ref[0, dx, pl.ds(start, rows), :]
    b = xs_ref[1, dx, pl.ds(start, rows), :]
    acc_ref[...] += jnp.dot(a, wa_ref[0, 0], preferred_element_type=jnp.float32) + jnp.dot(
        b, wb_ref[0, 0], preferred_element_type=jnp.float32
    )

    @pl.when(tap == 8)
    def _normalize():
        acc = acc_ref[...]
        count = rows * group
        total = jnp.broadcast_to(jnp.sum(acc, axis=0, keepdims=True), (8, acc.shape[1]))
        mean = group_sum(total, group)[0:1] / count
        d = acc - mean
        spread = jnp.broadcast_to(jnp.sum(d * d, axis=0, keepdims=True), (8, acc.shape[1]))
        variance = group_sum(spread, group)[0:1] / count
        v = d * lax.rsqrt(variance + EPS) * gain_ref[...] + shift_ref[...]
        o_ref[...] = (v / (1.0 + jnp.exp(-v))).astype(o_ref.dtype)


def conv_norm(frame, w_mine, w_other, gain, shift, side, width):
    rows, channels = frame.shape
    half = w_mine.shape[2]
    outputs = w_mine.shape[3]
    group = outputs // GROUPS
    kernel = functools.partial(conv_norm_kernel, width=width, group=group)
    weight_block = pl.BlockSpec((1, 1, half, outputs), lambda t, s: (t // 3, t % 3, 0, 0))
    return pl.pallas_call(
        kernel,
        out_shape=jax.ShapeDtypeStruct((rows, outputs), jnp.bfloat16),
        grid_spec=pltpu.PrefetchScalarGridSpec(
            num_scalar_prefetch=1,
            grid=(9,),
            in_specs=[
                pl.BlockSpec((rows, half), lambda t, s: (0, s[0])),
                pl.BlockSpec((rows, half), lambda t, s: (0, 1 - s[0])),
                weight_block,
                weight_block,
                pl.BlockSpec((1, outputs), lambda t, s: (0, 0)),
                pl.BlockSpec((1, outputs), lambda t, s: (0, 0)),
            ],
            out_specs=pl.BlockSpec((rows, outputs), lambda t, s: (0, 0)),
            scratch_shapes=[
                pltpu.VMEM((2, 3, rows + 2 * width, half), jnp.bfloat16),
                pltpu.VMEM((rows, outputs), jnp.float32),
            ],
        ),
        compiler_params=pltpu.CompilerParams(dimension_semantics=("arbitrary",)),
    )(side, frame, frame, w_mine, w_other, gain, shift)


def temporal_kernel(s_ref, ea, eb, pa, pb, ca, cb, cur_ref, wm_e, wo_e, wm_c, wo_c, wm_p, wo_p, o_ref):
    f32 = jnp.float32
    keep_edge = s_ref[1].astype(f32)
    keep_partner = s_ref[2].astype(f32)
    edge = jnp.dot(ea[...], wm_e[0], preferred_element_type=f32) + jnp.dot(
        eb[...], wo_e[0], preferred_element_type=f32
    )
    own = jnp.dot(ca[...], wm_c[0], preferred_element_type=f32) + jnp.dot(
        cb[...], wo_c[0], preferred_element_type=f32
    )
    partner = jnp.dot(pa[...], wm_p[0], preferred_element_type=f32) + jnp.dot(
        pb[...], wo_p[0], preferred_element_type=f32
    )
    total = own + keep_edge * edge + keep_partner * partner
    o_ref[...] = (cur_ref[...].astype(f32) + total).astype(o_ref.dtype)


def temporal(edge, partner, cur, w_mine, w_other, scalars):
    rows, channels = cur.shape
    half = w_mine.shape[1]
    outputs = w_mine.shape[2]
    mine = pl.BlockSpec((rows, half), lambda i, s: (0, s[0]))
    other = pl.BlockSpec((rows, half), lambda i, s: (0, 1 - s[0]))
    edge_tap = pl.BlockSpec((1, half, outputs), lambda i, s: (2 * s[0], 0, 0))
    own_tap = pl.BlockSpec((1, half, outputs), lambda i, s: (1, 0, 0))
    partner_tap = pl.BlockSpec((1, half, outputs), lambda i, s: (2 - 2 * s[0], 0, 0))
    return pl.pallas_call(
        temporal_kernel,
        out_shape=jax.ShapeDtypeStruct((rows, outputs), jnp.bfloat16),
        grid_spec=pltpu.PrefetchScalarGridSpec(
            num_scalar_prefetch=1,
            grid=(1,),
            in_specs=[
                mine, other, mine, other, mine, other,
                pl.BlockSpec((rows, outputs), lambda i, s: (0, 0)),
                edge_tap, edge_tap, own_tap, own_tap, partner_tap, partner_tap,
            ],
            out_specs=pl.BlockSpec((rows, outputs), lambda i, s: (0, 0)),
        ),
    )(scalars, edge, edge, partner, partner, cur, cur, cur,
      w_mine, w_other, w_mine, w_other, w_mine, w_other)


def body(video, w_spatial, norm_gain, norm_shift, w_time):
    count, height, width, channels = video.shape
    assert count == 1 and lax.axis_size("fsdp") == 2
    pixels = height * width
    side = lax.axis_index("fsdp")
    blocks = lax.axis_size("video") * 2
    position = lax.axis_index("video") * 2 + side

    route = []
    for j in range(blocks):
        target = j + 1 if j % 2 == 1 else j - 1
        if 0 <= target < blocks and min(j, target) % CLIP != CLIP - 1:
            route.append((j, target))
    frame = video.reshape(pixels, channels)
    edge_video = lax.ppermute(frame, ("video", "fsdp"), route)
    other_spatial = swap_pair(w_spatial)
    other_time = swap_pair(w_time)

    gain = norm_gain.reshape(1, channels)
    shift = norm_shift.reshape(1, channels)
    sides = side.reshape(1).astype(jnp.int32)
    hidden = conv_norm(frame, w_spatial, other_spatial, gain, shift, sides, width)
    partner = swap_pair(hidden)
    edge = conv_norm(edge_video, w_spatial, other_spatial, gain, shift, sides, width)

    keep_prev = (position % CLIP != 0).astype(jnp.int32)
    keep_next = (position % CLIP != CLIP - 1).astype(jnp.int32)
    keep_edge = jnp.where(side == 0, keep_prev, keep_next)
    keep_partner = jnp.where(side == 0, keep_next, keep_prev)
    scalars = jnp.stack([side.astype(jnp.int32), keep_edge, keep_partner])
    result = temporal(edge, partner, hidden, w_time, other_time, scalars)
    return result.reshape(count, height, width, channels)


def solution(mesh):
    placed = (
        P(("groups", "video", "fsdp"), None, None, None),
        P(None, None, "fsdp", None),
        P(),
        P(),
        P(None, "fsdp", None),
    )
    return jax.shard_map(
        body,
        mesh=mesh,
        in_specs=placed,
        out_specs=P(("groups", "video", "fsdp"), None, None, None),
        check_vma=False,
    )
```

```python
import functools

import jax
import jax.numpy as jnp
from jax import lax
from jax.experimental import pallas as pl
from jax.experimental.pallas import tpu as pltpu
from jax.sharding import PartitionSpec as P

GROUPS = 32
CLIP = 16
EPS = 1e-05


def swap_pair(block):
    return lax.ppermute(block, "fsdp", [(0, 1), (1, 0)])


def group_sum(row, size):
    lanes = lax.broadcasted_iota(jnp.int32, row.shape, 1)
    width = row.shape[1]
    step = 1
    while step < size:
        up = pltpu.roll(row, width - step, 1)
        down = pltpu.roll(row, step, 1)
        row = row + jnp.where((lanes & step) == 0, up, down)
        step *= 2
    return row


def conv_norm_kernel(side_ref, xa_ref, xb_ref, wa_ref, wb_ref, gain_ref, shift_ref, o_ref,
                     lhs_ref, *, width, group):
    rows, half = xa_ref.shape

    @pl.when(pl.program_id(0) == 0)
    def _prepare():
        col = lax.broadcasted_iota(jnp.int32, (rows, half), 0) % width
        zeros = jnp.zeros((width, half), jnp.bfloat16)
        for h, x_ref in enumerate((xa_ref, xb_ref)):
            xf = x_ref[...].astype(jnp.float32)
            left = jnp.where(col == 0, 0.0, pltpu.roll(xf, 1, 0)).astype(jnp.bfloat16)
            right = jnp.where(col == width - 1, 0.0, pltpu.roll(xf, rows - 1, 0)).astype(jnp.bfloat16)
            for dx, v in enumerate((left, xf.astype(jnp.bfloat16), right)):
                for dy in range(3):
                    lo = (dy * 3 + dx) * half
                    cols = slice(lo, lo + half)
                    if dy == 0:
                        lhs_ref[h, :width, cols] = zeros
                        lhs_ref[h, width:, cols] = v[: rows - width]
                    elif dy == 1:
                        lhs_ref[h, :, cols] = v
                    else:
                        lhs_ref[h, : rows - width, cols] = v[width:]
                        lhs_ref[h, rows - width :, cols] = zeros

    acc = jnp.dot(lhs_ref[0], wa_ref[...], preferred_element_type=jnp.float32) + jnp.dot(
        lhs_ref[1], wb_ref[...], preferred_element_type=jnp.float32
    )
    count = rows * group
    total = jnp.broadcast_to(jnp.sum(acc, axis=0, keepdims=True), (8, acc.shape[1]))
    mean = group_sum(total, group)[0:1] / count
    d = acc - mean
    spread = jnp.broadcast_to(jnp.sum(d * d, axis=0, keepdims=True), (8, acc.shape[1]))
    variance = group_sum(spread, group)[0:1] / count
    v = d * lax.rsqrt(variance + EPS) * gain_ref[...] + shift_ref[...]
    o_ref[...] = (v / (1.0 + jnp.exp(-v))).astype(o_ref.dtype)


def conv_norm(frame, w_mine, w_other, gain, shift, side, width, split=2):
    rows, channels = frame.shape
    half = w_mine.shape[2]
    outputs = w_mine.shape[3]
    group = outputs // GROUPS
    block = outputs // split
    kernel = functools.partial(conv_norm_kernel, width=width, group=group)
    weight_block = pl.BlockSpec((9 * half, block), lambda n, s: (0, n))
    row_block = pl.BlockSpec((1, block), lambda n, s: (0, n))
    return pl.pallas_call(
        kernel,
        out_shape=jax.ShapeDtypeStruct((rows, outputs), jnp.bfloat16),
        grid_spec=pltpu.PrefetchScalarGridSpec(
            num_scalar_prefetch=1,
            grid=(split,),
            in_specs=[
                pl.BlockSpec((rows, half), lambda n, s: (0, s[0])),
                pl.BlockSpec((rows, half), lambda n, s: (0, 1 - s[0])),
                weight_block,
                weight_block,
                row_block,
                row_block,
            ],
            out_specs=pl.BlockSpec((rows, block), lambda n, s: (0, n)),
            scratch_shapes=[pltpu.VMEM((2, rows, 9 * half), jnp.bfloat16)],
        ),
        compiler_params=pltpu.CompilerParams(dimension_semantics=("arbitrary",)),
    )(side, frame, frame, w_mine.reshape(9 * half, outputs), w_other.reshape(9 * half, outputs),
      gain, shift)


def temporal_kernel(s_ref, ea, eb, pa, pb, ca, cb, cur_ref, wm_ref, wo_ref, o_ref, lhs_ref):
    half = ea.shape[1]

    @pl.when(pl.program_id(0) == 0)
    def _prepare():
        keep_edge = s_ref[1] != 0
        keep_partner = s_ref[2] != 0
        for h, (e, p, c) in enumerate(((ea, pa, ca), (eb, pb, cb))):
            edge = jnp.where(keep_edge, e[...], jnp.zeros_like(e[...]))
            partner = jnp.where(keep_partner, p[...], jnp.zeros_like(p[...]))
            lhs_ref[h, :, half : 2 * half] = c[...]

            @pl.when(s_ref[0] == 0)
            def _():
                lhs_ref[h, :, :half] = edge
                lhs_ref[h, :, 2 * half :] = partner

            @pl.when(s_ref[0] != 0)
            def _():
                lhs_ref[h, :, :half] = partner
                lhs_ref[h, :, 2 * half :] = edge

    f32 = jnp.float32
    total = jnp.dot(lhs_ref[0], wm_ref[...], preferred_element_type=f32) + jnp.dot(
        lhs_ref[1], wo_ref[...], preferred_element_type=f32
    )
    o_ref[...] = (cur_ref[...].astype(f32) + total).astype(o_ref.dtype)


def temporal(edge, partner, cur, w_mine, w_other, scalars, split=2):
    rows, channels = cur.shape
    half = w_mine.shape[1]
    outputs = w_mine.shape[2]
    block = outputs // split
    mine = pl.BlockSpec((rows, half), lambda n, s: (0, s[0]))
    other = pl.BlockSpec((rows, half), lambda n, s: (0, 1 - s[0]))
    weight_block = pl.BlockSpec((3 * half, block), lambda n, s: (0, n))
    return pl.pallas_call(
        temporal_kernel,
        out_shape=jax.ShapeDtypeStruct((rows, outputs), jnp.bfloat16),
        grid_spec=pltpu.PrefetchScalarGridSpec(
            num_scalar_prefetch=1,
            grid=(split,),
            in_specs=[
                mine, other, mine, other, mine, other,
                pl.BlockSpec((rows, block), lambda n, s: (0, n)),
                weight_block, weight_block,
            ],
            out_specs=pl.BlockSpec((rows, block), lambda n, s: (0, n)),
            scratch_shapes=[pltpu.VMEM((2, rows, 3 * half), jnp.bfloat16)],
        ),
        compiler_params=pltpu.CompilerParams(dimension_semantics=("arbitrary",)),
    )(scalars, edge, edge, partner, partner, cur, cur, cur,
      w_mine.reshape(3 * half, outputs), w_other.reshape(3 * half, outputs))


def body(video, w_spatial, norm_gain, norm_shift, w_time):
    count, height, width, channels = video.shape
    assert count == 1 and lax.axis_size("fsdp") == 2
    pixels = height * width
    side = lax.axis_index("fsdp")
    blocks = lax.axis_size("video") * 2
    position = lax.axis_index("video") * 2 + side

    route = []
    for j in range(blocks):
        target = j + 1 if j % 2 == 1 else j - 1
        if 0 <= target < blocks and min(j, target) % CLIP != CLIP - 1:
            route.append((j, target))
    frame = video.reshape(pixels, channels)
    edge_video = lax.ppermute(frame, ("video", "fsdp"), route)
    other_spatial = swap_pair(w_spatial)
    other_time = swap_pair(w_time)

    gain = norm_gain.reshape(1, channels)
    shift = norm_shift.reshape(1, channels)
    sides = side.reshape(1).astype(jnp.int32)
    hidden = conv_norm(frame, w_spatial, other_spatial, gain, shift, sides, width)
    partner = swap_pair(hidden)
    edge = conv_norm(edge_video, w_spatial, other_spatial, gain, shift, sides, width)

    keep_prev = (position % CLIP != 0).astype(jnp.int32)
    keep_next = (position % CLIP != CLIP - 1).astype(jnp.int32)
    keep_edge = jnp.where(side == 0, keep_prev, keep_next)
    keep_partner = jnp.where(side == 0, keep_next, keep_prev)
    scalars = jnp.stack([side.astype(jnp.int32), keep_edge, keep_partner])
    result = temporal(edge, partner, hidden, w_time, other_time, scalars)
    return result.reshape(count, height, width, channels)


def solution(mesh):
    placed = (
        P(("groups", "video", "fsdp"), None, None, None),
        P(None, None, "fsdp", None),
        P(),
        P(),
        P(None, "fsdp", None),
    )
    return jax.shard_map(
        body,
        mesh=mesh,
        in_specs=placed,
        out_specs=P(("groups", "video", "fsdp"), None, None, None),
        check_vma=False,
    )
```

```python
import functools

import jax
import jax.numpy as jnp
from jax import lax
from jax.experimental import pallas as pl
from jax.experimental.pallas import tpu as pltpu
from jax.sharding import PartitionSpec as P

GROUPS = 32
CLIP = 16
EPS = 1e-05


def swap_pair(block):
    return lax.ppermute(block, "fsdp", [(0, 1), (1, 0)])


def group_sum(row, size):
    lanes = lax.broadcasted_iota(jnp.int32, row.shape, 1)
    width = row.shape[1]
    step = 1
    while step < size:
        up = pltpu.roll(row, width - step, 1)
        down = pltpu.roll(row, step, 1)
        row = row + jnp.where((lanes & step) == 0, up, down)
        step *= 2
    return row


def conv_norm_kernel(side_ref, xa_ref, xb_ref, wa_ref, wb_ref, gain_ref, shift_ref, o_ref,
                     lhs_ref, *, width, group):
    rows, half = xa_ref.shape

    @pl.when(pl.program_id(0) == 0)
    def _prepare():
        col = lax.broadcasted_iota(jnp.int32, (rows, half), 0) % width
        zeros = jnp.zeros((width, half), jnp.bfloat16)
        for h, x_ref in enumerate((xa_ref, xb_ref)):
            xf = x_ref[...].astype(jnp.float32)
            left = jnp.where(col == 0, 0.0, pltpu.roll(xf, 1, 0)).astype(jnp.bfloat16)
            right = jnp.where(col == width - 1, 0.0, pltpu.roll(xf, rows - 1, 0)).astype(jnp.bfloat16)
            for dx, v in enumerate((left, xf.astype(jnp.bfloat16), right)):
                for dy in range(3):
                    lo = (dy * 3 + dx) * half
                    cols = slice(lo, lo + half)
                    if dy == 0:
                        lhs_ref[h, :width, cols] = zeros
                        lhs_ref[h, width:, cols] = v[: rows - width]
                    elif dy == 1:
                        lhs_ref[h, :, cols] = v
                    else:
                        lhs_ref[h, : rows - width, cols] = v[width:]
                        lhs_ref[h, rows - width :, cols] = zeros

    acc = jnp.dot(lhs_ref[0], wa_ref[...], preferred_element_type=jnp.float32) + jnp.dot(
        lhs_ref[1], wb_ref[...], preferred_element_type=jnp.float32
    )
    count = rows * group
    total = jnp.broadcast_to(jnp.sum(acc, axis=0, keepdims=True), (8, acc.shape[1]))
    mean = group_sum(total, group)[0:1] / count
    d = acc - mean
    spread = jnp.broadcast_to(jnp.sum(d * d, axis=0, keepdims=True), (8, acc.shape[1]))
    variance = group_sum(spread, group)[0:1] / count
    v = d * lax.rsqrt(variance + EPS) * gain_ref[...] + shift_ref[...]
    o_ref[...] = (v / (1.0 + jnp.exp(-v))).astype(o_ref.dtype)


def conv_norm(frame, w_mine, w_other, gain, shift, side, width, split, part):
    rows, channels = frame.shape
    half = w_mine.shape[2]
    outputs = w_mine.shape[3]
    group = outputs // GROUPS
    block = outputs // split
    kernel = functools.partial(conv_norm_kernel, width=width, group=group)
    weight_block = pl.BlockSpec((9 * half, block), lambda n, s: (0, part))
    row_block = pl.BlockSpec((1, block), lambda n, s: (0, part))
    return pl.pallas_call(
        kernel,
        out_shape=jax.ShapeDtypeStruct((rows, block), jnp.bfloat16),
        grid_spec=pltpu.PrefetchScalarGridSpec(
            num_scalar_prefetch=1,
            grid=(1,),
            in_specs=[
                pl.BlockSpec((rows, half), lambda n, s: (0, s[0])),
                pl.BlockSpec((rows, half), lambda n, s: (0, 1 - s[0])),
                weight_block,
                weight_block,
                row_block,
                row_block,
            ],
            out_specs=pl.BlockSpec((rows, block), lambda n, s: (0, 0)),
            scratch_shapes=[pltpu.VMEM((2, rows, 9 * half), jnp.bfloat16)],
        ),
        compiler_params=pltpu.CompilerParams(dimension_semantics=("arbitrary",)),
    )(side, frame, frame, w_mine.reshape(9 * half, outputs), w_other.reshape(9 * half, outputs),
      gain, shift)


def temporal_kernel(s_ref, ea, eb, pa, pb, ca, cb, cur_ref, wm_ref, wo_ref, o_ref, lhs_ref):
    half = ea.shape[1]

    @pl.when(pl.program_id(0) == 0)
    def _prepare():
        keep_edge = s_ref[1] != 0
        keep_partner = s_ref[2] != 0
        for h, (e, p, c) in enumerate(((ea, pa, ca), (eb, pb, cb))):
            edge = jnp.where(keep_edge, e[...], jnp.zeros_like(e[...]))
            partner = jnp.where(keep_partner, p[...], jnp.zeros_like(p[...]))
            lhs_ref[h, :, half : 2 * half] = c[...]

            @pl.when(s_ref[0] == 0)
            def _():
                lhs_ref[h, :, :half] = edge
                lhs_ref[h, :, 2 * half :] = partner

            @pl.when(s_ref[0] != 0)
            def _():
                lhs_ref[h, :, :half] = partner
                lhs_ref[h, :, 2 * half :] = edge

    f32 = jnp.float32
    total = jnp.dot(lhs_ref[0], wm_ref[...], preferred_element_type=f32) + jnp.dot(
        lhs_ref[1], wo_ref[...], preferred_element_type=f32
    )
    o_ref[...] = (cur_ref[...].astype(f32) + total).astype(o_ref.dtype)


def temporal(edge, partner, cur, w_mine, w_other, scalars, split=2):
    rows, channels = cur.shape
    half = w_mine.shape[1]
    outputs = w_mine.shape[2]
    block = outputs // split
    mine = pl.BlockSpec((rows, half), lambda n, s: (0, s[0]))
    other = pl.BlockSpec((rows, half), lambda n, s: (0, 1 - s[0]))
    weight_block = pl.BlockSpec((3 * half, block), lambda n, s: (0, n))
    return pl.pallas_call(
        temporal_kernel,
        out_shape=jax.ShapeDtypeStruct((rows, outputs), jnp.bfloat16),
        grid_spec=pltpu.PrefetchScalarGridSpec(
            num_scalar_prefetch=1,
            grid=(split,),
            in_specs=[
                mine, other, mine, other, mine, other,
                pl.BlockSpec((rows, block), lambda n, s: (0, n)),
                weight_block, weight_block,
            ],
            out_specs=pl.BlockSpec((rows, block), lambda n, s: (0, n)),
            scratch_shapes=[pltpu.VMEM((2, rows, 3 * half), jnp.bfloat16)],
        ),
        compiler_params=pltpu.CompilerParams(dimension_semantics=("arbitrary",)),
    )(scalars, edge, edge, partner, partner, cur, cur, cur,
      w_mine.reshape(3 * half, outputs), w_other.reshape(3 * half, outputs))


def body(video, w_spatial, norm_gain, norm_shift, w_time):
    count, height, width, channels = video.shape
    assert count == 1 and lax.axis_size("fsdp") == 2
    pixels = height * width
    side = lax.axis_index("fsdp")
    blocks = lax.axis_size("video") * 2
    position = lax.axis_index("video") * 2 + side

    route = []
    for j in range(blocks):
        target = j + 1 if j % 2 == 1 else j - 1
        if 0 <= target < blocks and min(j, target) % CLIP != CLIP - 1:
            route.append((j, target))
    frame = video.reshape(pixels, channels)
    other_spatial = swap_pair(w_spatial)
    other_time = swap_pair(w_time)

    gain = norm_gain.reshape(1, channels)
    shift = norm_shift.reshape(1, channels)
    sides = side.reshape(1).astype(jnp.int32)
    split = 2
    pieces, edges, partners = [], [], []
    for part in range(split):
        piece = conv_norm(frame, w_spatial, other_spatial, gain, shift, sides, width, split, part)
        pieces.append(piece)
        edges.append(lax.ppermute(piece, ("video", "fsdp"), route))
        partners.append(swap_pair(piece))
    hidden = jnp.concatenate(pieces, axis=1)
    edge = jnp.concatenate(edges, axis=1)
    partner = jnp.concatenate(partners, axis=1)

    keep_prev = (position % CLIP != 0).astype(jnp.int32)
    keep_next = (position % CLIP != CLIP - 1).astype(jnp.int32)
    keep_edge = jnp.where(side == 0, keep_prev, keep_next)
    keep_partner = jnp.where(side == 0, keep_next, keep_prev)
    scalars = jnp.stack([side.astype(jnp.int32), keep_edge, keep_partner])
    result = temporal(edge, partner, hidden, w_time, other_time, scalars)
    return result.reshape(count, height, width, channels)


def solution(mesh):
    placed = (
        P(("groups", "video", "fsdp"), None, None, None),
        P(None, None, "fsdp", None),
        P(),
        P(),
        P(None, "fsdp", None),
    )
    return jax.shard_map(
        body,
        mesh=mesh,
        in_specs=placed,
        out_specs=P(("groups", "video", "fsdp"), None, None, None),
        check_vma=False,
    )
```

```python
import functools

import jax
import jax.numpy as jnp
from jax import lax
from jax.experimental import pallas as pl
from jax.experimental.pallas import tpu as pltpu
from jax.sharding import PartitionSpec as P

GROUPS = 32
CLIP = 16
EPS = 1e-05


def swap_pair(block):
    return lax.ppermute(block, "fsdp", [(0, 1), (1, 0)])


def group_sum(row, size):
    lanes = lax.broadcasted_iota(jnp.int32, row.shape, 1)
    width = row.shape[1]
    step = 1
    while step < size:
        up = pltpu.roll(row, width - step, 1)
        down = pltpu.roll(row, step, 1)
        row = row + jnp.where((lanes & step) == 0, up, down)
        step *= 2
    return row


def conv_norm_kernel(side_ref, xa_ref, xb_ref, wa_ref, wb_ref, gain_ref, shift_ref, o_ref,
                     lhs_ref, *, width, group):
    rows, half = xa_ref.shape

    @pl.when(pl.program_id(0) == 0)
    def _prepare():
        col = lax.broadcasted_iota(jnp.int32, (rows, half), 0) % width
        zeros = jnp.zeros((width, half), jnp.bfloat16)
        for h, x_ref in enumerate((xa_ref, xb_ref)):
            xf = x_ref[...].astype(jnp.float32)
            left = jnp.where(col == 0, 0.0, pltpu.roll(xf, 1, 0)).astype(jnp.bfloat16)
            right = jnp.where(col == width - 1, 0.0, pltpu.roll(xf, rows - 1, 0)).astype(jnp.bfloat16)
            for dx, v in enumerate((left, xf.astype(jnp.bfloat16), right)):
                for dy in range(3):
                    lo = (dy * 3 + dx) * half
                    cols = slice(lo, lo + half)
                    if dy == 0:
                        lhs_ref[h, :width, cols] = zeros
                        lhs_ref[h, width:, cols] = v[: rows - width]
                    elif dy == 1:
                        lhs_ref[h, :, cols] = v
                    else:
                        lhs_ref[h, : rows - width, cols] = v[width:]
                        lhs_ref[h, rows - width :, cols] = zeros

    acc = jnp.dot(lhs_ref[0], wa_ref[...], preferred_element_type=jnp.float32) + jnp.dot(
        lhs_ref[1], wb_ref[...], preferred_element_type=jnp.float32
    )
    count = rows * group
    total = jnp.broadcast_to(jnp.sum(acc, axis=0, keepdims=True), (8, acc.shape[1]))
    mean = group_sum(total, group)[0:1] / count
    d = acc - mean
    spread = jnp.broadcast_to(jnp.sum(d * d, axis=0, keepdims=True), (8, acc.shape[1]))
    variance = group_sum(spread, group)[0:1] / count
    v = d * lax.rsqrt(variance + EPS) * gain_ref[...] + shift_ref[...]
    o_ref[...] = (v / (1.0 + jnp.exp(-v))).astype(o_ref.dtype)


def conv_norm(frame, w_mine, w_other, gain, shift, side, width, split=2):
    rows, channels = frame.shape
    half = w_mine.shape[2]
    outputs = w_mine.shape[3]
    group = outputs // GROUPS
    block = outputs // split
    kernel = functools.partial(conv_norm_kernel, width=width, group=group)
    weight_block = pl.BlockSpec((9 * half, block), lambda n, s: (0, n))
    row_block = pl.BlockSpec((1, block), lambda n, s: (0, n))
    return pl.pallas_call(
        kernel,
        out_shape=jax.ShapeDtypeStruct((rows, outputs), jnp.bfloat16),
        grid_spec=pltpu.PrefetchScalarGridSpec(
            num_scalar_prefetch=1,
            grid=(split,),
            in_specs=[
                pl.BlockSpec((rows, half), lambda n, s: (0, s[0])),
                pl.BlockSpec((rows, half), lambda n, s: (0, 1 - s[0])),
                weight_block,
                weight_block,
                row_block,
                row_block,
            ],
            out_specs=pl.BlockSpec((rows, block), lambda n, s: (0, n)),
            scratch_shapes=[pltpu.VMEM((2, rows, 9 * half), jnp.bfloat16)],
        ),
        compiler_params=pltpu.CompilerParams(dimension_semantics=("arbitrary",)),
    )(side, frame, frame, w_mine.reshape(9 * half, outputs), w_other.reshape(9 * half, outputs),
      gain, shift)


def temporal_kernel(s_ref, ea, eb, pa, pb, ca, cb, cur_ref, wm_ref, wo_ref, o_ref, lhs_ref):
    half = ea.shape[1]

    @pl.when(pl.program_id(0) == 0)
    def _prepare():
        keep_edge = s_ref[1] != 0
        keep_partner = s_ref[2] != 0
        for h, (e, p, c) in enumerate(((ea, pa, ca), (eb, pb, cb))):
            edge = jnp.where(keep_edge, e[...], jnp.zeros_like(e[...]))
            partner = jnp.where(keep_partner, p[...], jnp.zeros_like(p[...]))
            lhs_ref[h, :, half : 2 * half] = c[...]

            @pl.when(s_ref[0] == 0)
            def _():
                lhs_ref[h, :, :half] = edge
                lhs_ref[h, :, 2 * half :] = partner

            @pl.when(s_ref[0] != 0)
            def _():
                lhs_ref[h, :, :half] = partner
                lhs_ref[h, :, 2 * half :] = edge

    f32 = jnp.float32
    total = jnp.dot(lhs_ref[0], wm_ref[...], preferred_element_type=f32) + jnp.dot(
        lhs_ref[1], wo_ref[...], preferred_element_type=f32
    )
    o_ref[...] = (cur_ref[...].astype(f32) + total).astype(o_ref.dtype)


def temporal(edge, partner, cur, w_mine, w_other, scalars, split=2):
    rows, channels = cur.shape
    half = w_mine.shape[1]
    outputs = w_mine.shape[2]
    block = outputs // split
    mine = pl.BlockSpec((rows, half), lambda n, s: (0, s[0]))
    other = pl.BlockSpec((rows, half), lambda n, s: (0, 1 - s[0]))
    weight_block = pl.BlockSpec((3 * half, block), lambda n, s: (0, n))
    return pl.pallas_call(
        temporal_kernel,
        out_shape=jax.ShapeDtypeStruct((rows, outputs), jnp.bfloat16),
        grid_spec=pltpu.PrefetchScalarGridSpec(
            num_scalar_prefetch=1,
            grid=(split,),
            in_specs=[
                mine, other, mine, other, mine, other,
                pl.BlockSpec((rows, block), lambda n, s: (0, n)),
                weight_block, weight_block,
            ],
            out_specs=pl.BlockSpec((rows, block), lambda n, s: (0, n)),
            scratch_shapes=[pltpu.VMEM((2, rows, 3 * half), jnp.bfloat16)],
        ),
        compiler_params=pltpu.CompilerParams(dimension_semantics=("arbitrary",)),
    )(scalars, edge, edge, partner, partner, cur, cur, cur,
      w_mine.reshape(3 * half, outputs), w_other.reshape(3 * half, outputs))


def body(video, w_spatial, norm_gain, norm_shift, w_time):
    count, height, width, channels = video.shape
    assert count == 1 and lax.axis_size("fsdp") == 2
    pixels = height * width
    side = lax.axis_index("fsdp")
    blocks = lax.axis_size("video") * 2
    position = lax.axis_index("video") * 2 + side

    route = []
    for j in range(blocks):
        target = j + 1 if j % 2 == 1 else j - 1
        if 0 <= target < blocks and min(j, target) % CLIP != CLIP - 1:
            route.append((j, target))
    frame = video.reshape(pixels, channels)
    other_spatial = swap_pair(w_spatial)
    other_time = swap_pair(w_time)

    gain = norm_gain.reshape(1, channels)
    shift = norm_shift.reshape(1, channels)
    sides = side.reshape(1).astype(jnp.int32)
    hidden = conv_norm(frame, w_spatial, other_spatial, gain, shift, sides, width)
    edge = lax.ppermute(hidden, ("video", "fsdp"), route)
    partner = swap_pair(hidden)

    keep_prev = (position % CLIP != 0).astype(jnp.int32)
    keep_next = (position % CLIP != CLIP - 1).astype(jnp.int32)
    keep_edge = jnp.where(side == 0, keep_prev, keep_next)
    keep_partner = jnp.where(side == 0, keep_next, keep_prev)
    scalars = jnp.stack([side.astype(jnp.int32), keep_edge, keep_partner])
    result = temporal(edge, partner, hidden, w_time, other_time, scalars)
    return result.reshape(count, height, width, channels)


def solution(mesh):
    placed = (
        P(("groups", "video", "fsdp"), None, None, None),
        P(None, None, "fsdp", None),
        P(),
        P(),
        P(None, "fsdp", None),
    )
    return jax.shard_map(
        body,
        mesh=mesh,
        in_specs=placed,
        out_specs=P(("groups", "video", "fsdp"), None, None, None),
        check_vma=False,
    )
```

```python
import functools

import jax
import jax.numpy as jnp
from jax import lax
from jax.experimental import pallas as pl
from jax.experimental.pallas import tpu as pltpu
from jax.sharding import PartitionSpec as P

GROUPS = 32
CLIP = 16
EPS = 1e-05


def swap_pair(block):
    return lax.ppermute(block, "fsdp", [(0, 1), (1, 0)])


def group_sum(row, size):
    lanes = lax.broadcasted_iota(jnp.int32, row.shape, 1)
    width = row.shape[1]
    step = 1
    while step < size:
        up = pltpu.roll(row, width - step, 1)
        down = pltpu.roll(row, step, 1)
        row = row + jnp.where((lanes & step) == 0, up, down)
        step *= 2
    return row


def conv_norm_kernel(side_ref, lo_ref, hi_ref, wa_ref, wb_ref, gain_ref, shift_ref, o_ref,
                     lhs_ref, *, width, group):
    rows, half = lo_ref.shape

    @pl.when(pl.program_id(0) == 0)
    def _prepare():
        col = lax.broadcasted_iota(jnp.int32, (rows, half), 0) % width
        zeros = jnp.zeros((width, half), jnp.bfloat16)
        for h, x_ref in enumerate((lo_ref, hi_ref)):
            slot = (h + side_ref[0]) % 2
            xf = x_ref[...].astype(jnp.float32)
            left = jnp.where(col == 0, 0.0, pltpu.roll(xf, 1, 0)).astype(jnp.bfloat16)
            right = jnp.where(col == width - 1, 0.0, pltpu.roll(xf, rows - 1, 0)).astype(jnp.bfloat16)
            for dx, v in enumerate((left, xf.astype(jnp.bfloat16), right)):
                for dy in range(3):
                    lo = (dy * 3 + dx) * half
                    cols = slice(lo, lo + half)
                    if dy == 0:
                        lhs_ref[slot, :width, cols] = zeros
                        lhs_ref[slot, width:, cols] = v[: rows - width]
                    elif dy == 1:
                        lhs_ref[slot, :, cols] = v
                    else:
                        lhs_ref[slot, : rows - width, cols] = v[width:]
                        lhs_ref[slot, rows - width :, cols] = zeros

    acc = jnp.dot(lhs_ref[0], wa_ref[...], preferred_element_type=jnp.float32) + jnp.dot(
        lhs_ref[1], wb_ref[...], preferred_element_type=jnp.float32
    )
    count = rows * group
    total = jnp.broadcast_to(jnp.sum(acc, axis=0, keepdims=True), (8, acc.shape[1]))
    mean = group_sum(total, group)[0:1] / count
    d = acc - mean
    spread = jnp.broadcast_to(jnp.sum(d * d, axis=0, keepdims=True), (8, acc.shape[1]))
    variance = group_sum(spread, group)[0:1] / count
    v = d * lax.rsqrt(variance + EPS) * gain_ref[...] + shift_ref[...]
    o_ref[...] = (v / (1.0 + jnp.exp(-v))).astype(o_ref.dtype)


def conv_norm(lo, hi, w_mine, w_other, gain, shift, side, width, split=2):
    rows = lo.shape[0]
    half = w_mine.shape[2]
    hi_block = 1 if hi.shape[1] > half else 0
    outputs = w_mine.shape[3]
    group = outputs // GROUPS
    block = outputs // split
    kernel = functools.partial(conv_norm_kernel, width=width, group=group)
    weight_block = pl.BlockSpec((9 * half, block), lambda n, s: (0, n))
    row_block = pl.BlockSpec((1, block), lambda n, s: (0, n))
    return pl.pallas_call(
        kernel,
        out_shape=jax.ShapeDtypeStruct((rows, outputs), jnp.bfloat16),
        grid_spec=pltpu.PrefetchScalarGridSpec(
            num_scalar_prefetch=1,
            grid=(split,),
            in_specs=[
                pl.BlockSpec((rows, half), lambda n, s: (0, 0)),
                pl.BlockSpec((rows, half), lambda n, s: (0, hi_block)),
                weight_block,
                weight_block,
                row_block,
                row_block,
            ],
            out_specs=pl.BlockSpec((rows, block), lambda n, s: (0, n)),
            scratch_shapes=[pltpu.VMEM((2, rows, 9 * half), jnp.bfloat16)],
        ),
        compiler_params=pltpu.CompilerParams(dimension_semantics=("arbitrary",)),
    )(side, lo, hi, w_mine.reshape(9 * half, outputs), w_other.reshape(9 * half, outputs),
      gain, shift)


def temporal_kernel(s_ref, ea, eb, pa, pb, ca, cb, cur_ref, wm_ref, wo_ref, o_ref, lhs_ref):
    half = ea.shape[1]

    @pl.when(pl.program_id(0) == 0)
    def _prepare():
        keep_edge = s_ref[1] != 0
        keep_partner = s_ref[2] != 0
        for h, (e, p, c) in enumerate(((ea, pa, ca), (eb, pb, cb))):
            edge = jnp.where(keep_edge, e[...], jnp.zeros_like(e[...]))
            partner = jnp.where(keep_partner, p[...], jnp.zeros_like(p[...]))
            lhs_ref[h, :, half : 2 * half] = c[...]

            @pl.when(s_ref[0] == 0)
            def _():
                lhs_ref[h, :, :half] = edge
                lhs_ref[h, :, 2 * half :] = partner

            @pl.when(s_ref[0] != 0)
            def _():
                lhs_ref[h, :, :half] = partner
                lhs_ref[h, :, 2 * half :] = edge

    f32 = jnp.float32
    total = jnp.dot(lhs_ref[0], wm_ref[...], preferred_element_type=f32) + jnp.dot(
        lhs_ref[1], wo_ref[...], preferred_element_type=f32
    )
    o_ref[...] = (cur_ref[...].astype(f32) + total).astype(o_ref.dtype)


def temporal(edge, partner, cur, w_mine, w_other, scalars, split=2):
    rows, channels = cur.shape
    half = w_mine.shape[1]
    outputs = w_mine.shape[2]
    block = outputs // split
    mine = pl.BlockSpec((rows, half), lambda n, s: (0, s[0]))
    other = pl.BlockSpec((rows, half), lambda n, s: (0, 1 - s[0]))
    weight_block = pl.BlockSpec((3 * half, block), lambda n, s: (0, n))
    return pl.pallas_call(
        temporal_kernel,
        out_shape=jax.ShapeDtypeStruct((rows, outputs), jnp.bfloat16),
        grid_spec=pltpu.PrefetchScalarGridSpec(
            num_scalar_prefetch=1,
            grid=(split,),
            in_specs=[
                mine, other, mine, other, mine, other,
                pl.BlockSpec((rows, block), lambda n, s: (0, n)),
                weight_block, weight_block,
            ],
            out_specs=pl.BlockSpec((rows, block), lambda n, s: (0, n)),
            scratch_shapes=[pltpu.VMEM((2, rows, 3 * half), jnp.bfloat16)],
        ),
        compiler_params=pltpu.CompilerParams(dimension_semantics=("arbitrary",)),
    )(scalars, edge, edge, partner, partner, cur, cur, cur,
      w_mine.reshape(3 * half, outputs), w_other.reshape(3 * half, outputs))


def body(video, w_spatial, norm_gain, norm_shift, w_time):
    count, height, width, channels = video.shape
    assert count == 1 and lax.axis_size("fsdp") == 2
    pixels = height * width
    side = lax.axis_index("fsdp")
    blocks = lax.axis_size("video") * 2
    position = lax.axis_index("video") * 2 + side

    route = []
    for j in range(blocks):
        target = j + 1 if j % 2 == 1 else j - 1
        if 0 <= target < blocks and min(j, target) % CLIP != CLIP - 1:
            route.append((j, target))
    frame = video.reshape(pixels, channels)
    half = channels // 2
    edge_lo = lax.ppermute(frame[:, :half], ("video", "fsdp"), route)
    edge_hi = lax.ppermute(frame[:, half:], ("video", "fsdp"), route)
    other_spatial = swap_pair(w_spatial)
    other_time = swap_pair(w_time)

    gain = norm_gain.reshape(1, channels)
    shift = norm_shift.reshape(1, channels)
    sides = side.reshape(1).astype(jnp.int32)
    hidden = conv_norm(frame, frame, w_spatial, other_spatial, gain, shift, sides, width)
    partner = swap_pair(hidden)
    edge = conv_norm(edge_lo, edge_hi, w_spatial, other_spatial, gain, shift, sides, width)

    keep_prev = (position % CLIP != 0).astype(jnp.int32)
    keep_next = (position % CLIP != CLIP - 1).astype(jnp.int32)
    keep_edge = jnp.where(side == 0, keep_prev, keep_next)
    keep_partner = jnp.where(side == 0, keep_next, keep_prev)
    scalars = jnp.stack([side.astype(jnp.int32), keep_edge, keep_partner])
    result = temporal(edge, partner, hidden, w_time, other_time, scalars)
    return result.reshape(count, height, width, channels)


def solution(mesh):
    placed = (
        P(("groups", "video", "fsdp"), None, None, None),
        P(None, None, "fsdp", None),
        P(),
        P(),
        P(None, "fsdp", None),
    )
    return jax.shard_map(
        body,
        mesh=mesh,
        in_specs=placed,
        out_specs=P(("groups", "video", "fsdp"), None, None, None),
        check_vma=False,
    )
```

```python
import functools

import jax
import jax.numpy as jnp
from jax import lax
from jax.experimental import pallas as pl
from jax.experimental.pallas import tpu as pltpu
from jax.sharding import PartitionSpec as P

GROUPS = 32
CLIP = 16
EPS = 1e-05


def swap_pair(block):
    return lax.ppermute(block, "fsdp", [(0, 1), (1, 0)])


def group_sum(row, size):
    lanes = lax.broadcasted_iota(jnp.int32, row.shape, 1)
    width = row.shape[1]
    step = 1
    while step < size:
        up = pltpu.roll(row, width - step, 1)
        down = pltpu.roll(row, step, 1)
        row = row + jnp.where((lanes & step) == 0, up, down)
        step *= 2
    return row


def conv_norm_kernel(side_ref, xa_ref, xb_ref, wa_ref, wb_ref, gain_ref, shift_ref, o_ref,
                     lhs_ref, *, width, group):
    rows, half = xa_ref.shape

    @pl.when(pl.program_id(0) == 0)
    def _prepare():
        col = lax.broadcasted_iota(jnp.int32, (rows, half), 0) % width
        zeros = jnp.zeros((width, half), jnp.bfloat16)
        for h, x_ref in enumerate((xa_ref, xb_ref)):
            xf = x_ref[...].astype(jnp.float32)
            left = jnp.where(col == 0, 0.0, pltpu.roll(xf, 1, 0)).astype(jnp.bfloat16)
            right = jnp.where(col == width - 1, 0.0, pltpu.roll(xf, rows - 1, 0)).astype(jnp.bfloat16)
            for dx, v in enumerate((left, xf.astype(jnp.bfloat16), right)):
                for dy in range(3):
                    lo = (dy * 3 + dx) * half
                    cols = slice(lo, lo + half)
                    if dy == 0:
                        lhs_ref[h, :width, cols] = zeros
                        lhs_ref[h, width:, cols] = v[: rows - width]
                    elif dy == 1:
                        lhs_ref[h, :, cols] = v
                    else:
                        lhs_ref[h, : rows - width, cols] = v[width:]
                        lhs_ref[h, rows - width :, cols] = zeros

    acc = jnp.dot(lhs_ref[0], wa_ref[...], preferred_element_type=jnp.float32) + jnp.dot(
        lhs_ref[1], wb_ref[...], preferred_element_type=jnp.float32
    )
    count = rows * group
    total = jnp.broadcast_to(jnp.sum(acc, axis=0, keepdims=True), (8, acc.shape[1]))
    mean = group_sum(total, group)[0:1] / count
    d = acc - mean
    spread = jnp.broadcast_to(jnp.sum(d * d, axis=0, keepdims=True), (8, acc.shape[1]))
    variance = group_sum(spread, group)[0:1] / count
    v = d * lax.rsqrt(variance + EPS) * gain_ref[...] + shift_ref[...]
    o_ref[...] = (v / (1.0 + jnp.exp(-v))).astype(o_ref.dtype)


def conv_norm(frame, w_mine, w_other, gain, shift, side, width, split=1):
    rows, channels = frame.shape
    half = w_mine.shape[2]
    outputs = w_mine.shape[3]
    group = outputs // GROUPS
    block = outputs // split
    kernel = functools.partial(conv_norm_kernel, width=width, group=group)
    weight_block = pl.BlockSpec((9 * half, block), lambda n, s: (0, n))
    row_block = pl.BlockSpec((1, block), lambda n, s: (0, n))
    return pl.pallas_call(
        kernel,
        out_shape=jax.ShapeDtypeStruct((rows, outputs), jnp.bfloat16),
        grid_spec=pltpu.PrefetchScalarGridSpec(
            num_scalar_prefetch=1,
            grid=(split,),
            in_specs=[
                pl.BlockSpec((rows, half), lambda n, s: (0, s[0])),
                pl.BlockSpec((rows, half), lambda n, s: (0, 1 - s[0])),
                weight_block,
                weight_block,
                row_block,
                row_block,
            ],
            out_specs=pl.BlockSpec((rows, block), lambda n, s: (0, n)),
            scratch_shapes=[pltpu.VMEM((2, rows, 9 * half), jnp.bfloat16)],
        ),
        compiler_params=pltpu.CompilerParams(dimension_semantics=("arbitrary",)),
    )(side, frame, frame, w_mine.reshape(9 * half, outputs), w_other.reshape(9 * half, outputs),
      gain, shift)


def temporal_kernel(s_ref, ea, eb, pa, pb, ca, cb, cur_ref, wm_ref, wo_ref, o_ref, lhs_ref):
    half = ea.shape[1]

    @pl.when(pl.program_id(0) == 0)
    def _prepare():
        keep_edge = s_ref[1] != 0
        keep_partner = s_ref[2] != 0
        for h, (e, p, c) in enumerate(((ea, pa, ca), (eb, pb, cb))):
            edge = jnp.where(keep_edge, e[...], jnp.zeros_like(e[...]))
            partner = jnp.where(keep_partner, p[...], jnp.zeros_like(p[...]))
            lhs_ref[h, :, half : 2 * half] = c[...]

            @pl.when(s_ref[0] == 0)
            def _():
                lhs_ref[h, :, :half] = edge
                lhs_ref[h, :, 2 * half :] = partner

            @pl.when(s_ref[0] != 0)
            def _():
                lhs_ref[h, :, :half] = partner
                lhs_ref[h, :, 2 * half :] = edge

    f32 = jnp.float32
    total = jnp.dot(lhs_ref[0], wm_ref[...], preferred_element_type=f32) + jnp.dot(
        lhs_ref[1], wo_ref[...], preferred_element_type=f32
    )
    o_ref[...] = (cur_ref[...].astype(f32) + total).astype(o_ref.dtype)


def temporal(edge, partner, cur, w_mine, w_other, scalars, split=2):
    rows, channels = cur.shape
    half = w_mine.shape[1]
    outputs = w_mine.shape[2]
    block = outputs // split
    mine = pl.BlockSpec((rows, half), lambda n, s: (0, s[0]))
    other = pl.BlockSpec((rows, half), lambda n, s: (0, 1 - s[0]))
    weight_block = pl.BlockSpec((3 * half, block), lambda n, s: (0, n))
    return pl.pallas_call(
        temporal_kernel,
        out_shape=jax.ShapeDtypeStruct((rows, outputs), jnp.bfloat16),
        grid_spec=pltpu.PrefetchScalarGridSpec(
            num_scalar_prefetch=1,
            grid=(split,),
            in_specs=[
                mine, other, mine, other, mine, other,
                pl.BlockSpec((rows, block), lambda n, s: (0, n)),
                weight_block, weight_block,
            ],
            out_specs=pl.BlockSpec((rows, block), lambda n, s: (0, n)),
            scratch_shapes=[pltpu.VMEM((2, rows, 3 * half), jnp.bfloat16)],
        ),
        compiler_params=pltpu.CompilerParams(dimension_semantics=("arbitrary",)),
    )(scalars, edge, edge, partner, partner, cur, cur, cur,
      w_mine.reshape(3 * half, outputs), w_other.reshape(3 * half, outputs))


def body(video, w_spatial, norm_gain, norm_shift, w_time):
    count, height, width, channels = video.shape
    assert count == 1 and lax.axis_size("fsdp") == 2
    pixels = height * width
    side = lax.axis_index("fsdp")
    blocks = lax.axis_size("video") * 2
    position = lax.axis_index("video") * 2 + side

    route = []
    for j in range(blocks):
        target = j + 1 if j % 2 == 1 else j - 1
        if 0 <= target < blocks and min(j, target) % CLIP != CLIP - 1:
            route.append((j, target))
    frame = video.reshape(pixels, channels)
    edge_video = lax.ppermute(frame, ("video", "fsdp"), route)
    other_spatial = swap_pair(w_spatial)
    other_time = swap_pair(w_time)

    gain = norm_gain.reshape(1, channels)
    shift = norm_shift.reshape(1, channels)
    sides = side.reshape(1).astype(jnp.int32)
    hidden = conv_norm(frame, w_spatial, other_spatial, gain, shift, sides, width)
    partner = swap_pair(hidden)
    edge = conv_norm(edge_video, w_spatial, other_spatial, gain, shift, sides, width)

    keep_prev = (position % CLIP != 0).astype(jnp.int32)
    keep_next = (position % CLIP != CLIP - 1).astype(jnp.int32)
    keep_edge = jnp.where(side == 0, keep_prev, keep_next)
    keep_partner = jnp.where(side == 0, keep_next, keep_prev)
    scalars = jnp.stack([side.astype(jnp.int32), keep_edge, keep_partner])
    result = temporal(edge, partner, hidden, w_time, other_time, scalars)
    return result.reshape(count, height, width, channels)


def solution(mesh):
    placed = (
        P(("groups", "video", "fsdp"), None, None, None),
        P(None, None, "fsdp", None),
        P(),
        P(),
        P(None, "fsdp", None),
    )
    return jax.shard_map(
        body,
        mesh=mesh,
        in_specs=placed,
        out_specs=P(("groups", "video", "fsdp"), None, None, None),
        check_vma=False,
    )
```

```python
import functools

import jax
import jax.numpy as jnp
from jax import lax
from jax.experimental import pallas as pl
from jax.experimental.pallas import tpu as pltpu
from jax.sharding import PartitionSpec as P

GROUPS = 32
CLIP = 16
EPS = 1e-05


def swap_pair(block):
    return lax.ppermute(block, "fsdp", [(0, 1), (1, 0)])


def group_sum(row, size):
    lanes = lax.broadcasted_iota(jnp.int32, row.shape, 1)
    width = row.shape[1]
    step = 1
    while step < size:
        up = pltpu.roll(row, width - step, 1)
        down = pltpu.roll(row, step, 1)
        row = row + jnp.where((lanes & step) == 0, up, down)
        step *= 2
    return row


def conv_norm_kernel(side_ref, xa_ref, xb_ref, wa_ref, wb_ref, gain_ref, shift_ref, o_ref,
                     lhs_ref, *, width, group):
    rows, half = xa_ref.shape

    @pl.when(pl.program_id(0) == 0)
    def _prepare():
        col = lax.broadcasted_iota(jnp.int32, (rows, half), 0) % width
        zeros = jnp.zeros((width, half), jnp.bfloat16)
        for h, x_ref in enumerate((xa_ref, xb_ref)):
            xf = x_ref[...].astype(jnp.float32)
            left = jnp.where(col == 0, 0.0, pltpu.roll(xf, 1, 0)).astype(jnp.bfloat16)
            right = jnp.where(col == width - 1, 0.0, pltpu.roll(xf, rows - 1, 0)).astype(jnp.bfloat16)
            for dx, v in enumerate((left, xf.astype(jnp.bfloat16), right)):
                for dy in range(3):
                    lo = (dy * 3 + dx) * half
                    cols = slice(lo, lo + half)
                    if dy == 0:
                        lhs_ref[h, :width, cols] = zeros
                        lhs_ref[h, width:, cols] = v[: rows - width]
                    elif dy == 1:
                        lhs_ref[h, :, cols] = v
                    else:
                        lhs_ref[h, : rows - width, cols] = v[width:]
                        lhs_ref[h, rows - width :, cols] = zeros

    acc = jnp.dot(lhs_ref[0], wa_ref[...], preferred_element_type=jnp.float32) + jnp.dot(
        lhs_ref[1], wb_ref[...], preferred_element_type=jnp.float32
    )
    count = rows * group
    total = jnp.broadcast_to(jnp.sum(acc, axis=0, keepdims=True), (8, acc.shape[1]))
    mean = group_sum(total, group)[0:1] / count
    d = acc - mean
    spread = jnp.broadcast_to(jnp.sum(d * d, axis=0, keepdims=True), (8, acc.shape[1]))
    variance = group_sum(spread, group)[0:1] / count
    v = d * lax.rsqrt(variance + EPS) * gain_ref[...] + shift_ref[...]
    o_ref[...] = (v / (1.0 + jnp.exp(-v))).astype(o_ref.dtype)


def conv_norm(frame, w_mine, w_other, gain, shift, side, width, split=1):
    rows, channels = frame.shape
    half = w_mine.shape[2]
    outputs = w_mine.shape[3]
    group = outputs // GROUPS
    block = outputs // split
    kernel = functools.partial(conv_norm_kernel, width=width, group=group)
    weight_block = pl.BlockSpec((9 * half, block), lambda n, s: (0, n))
    row_block = pl.BlockSpec((1, block), lambda n, s: (0, n))
    return pl.pallas_call(
        kernel,
        out_shape=jax.ShapeDtypeStruct((rows, outputs), jnp.bfloat16),
        grid_spec=pltpu.PrefetchScalarGridSpec(
            num_scalar_prefetch=1,
            grid=(split,),
            in_specs=[
                pl.BlockSpec((rows, half), lambda n, s: (0, s[0])),
                pl.BlockSpec((rows, half), lambda n, s: (0, 1 - s[0])),
                weight_block,
                weight_block,
                row_block,
                row_block,
            ],
            out_specs=pl.BlockSpec((rows, block), lambda n, s: (0, n)),
            scratch_shapes=[pltpu.VMEM((2, rows, 9 * half), jnp.bfloat16)],
        ),
        compiler_params=pltpu.CompilerParams(dimension_semantics=("arbitrary",)),
    )(side, frame, frame, w_mine.reshape(9 * half, outputs), w_other.reshape(9 * half, outputs),
      gain, shift)


def edge_temporal_kernel(s_ref, xa_ref, xb_ref, wa_ref, wb_ref, gain_ref, shift_ref,
                         cur_hbm, partner_hbm, wtm_hbm, wto_hbm, o_ref,
                         lhs_ref, edge_v, cur_v, partner_v, wtm_v, wto_v, tl_ref, sem,
                         *, width, group):
    copies = [
        pltpu.make_async_copy(src, dst, sem.at[i])
        for i, (src, dst) in enumerate(
            ((cur_hbm, cur_v), (partner_hbm, partner_v), (wtm_hbm, wtm_v), (wto_hbm, wto_v))
        )
    ]
    for copy in copies:
        copy.start()
    conv_norm_kernel(s_ref, xa_ref, xb_ref, wa_ref, wb_ref, gain_ref, shift_ref, edge_v,
                     lhs_ref, width=width, group=group)
    for copy in copies:
        copy.wait()

    rows, half = xa_ref.shape
    keep_edge = s_ref[1] != 0
    keep_partner = s_ref[2] != 0
    for side in range(2):
        @pl.when(s_ref[0] == side)
        def _fill():
            mine = slice(side * half, (side + 1) * half)
            other = slice((1 - side) * half, (2 - side) * half)
            for h, cols in enumerate((mine, other)):
                e = edge_v[:, cols]
                p = partner_v[:, cols]
                e = jnp.where(keep_edge, e, jnp.zeros_like(e))
                p = jnp.where(keep_partner, p, jnp.zeros_like(p))
                before, after = (e, p) if side == 0 else (p, e)
                tl_ref[h, :, :half] = before
                tl_ref[h, :, half : 2 * half] = cur_v[:, cols]
                tl_ref[h, :, 2 * half :] = after

    f32 = jnp.float32
    total = jnp.dot(tl_ref[0], wtm_v[...], preferred_element_type=f32) + jnp.dot(
        tl_ref[1], wto_v[...], preferred_element_type=f32
    )
    o_ref[...] = (cur_v[...].astype(f32) + total).astype(o_ref.dtype)


def edge_temporal(frame, w_mine, w_other, gain, shift, cur, partner, t_mine, t_other, scalars,
                  width):
    rows, channels = frame.shape
    half = w_mine.shape[2]
    outputs = w_mine.shape[3]
    group = outputs // GROUPS
    kernel = functools.partial(edge_temporal_kernel, width=width, group=group)
    weight_block = pl.BlockSpec((9 * half, outputs), lambda n, s: (0, 0))
    row_block = pl.BlockSpec((1, outputs), lambda n, s: (0, 0))
    anywhere = pl.BlockSpec(memory_space=pl.ANY)
    return pl.pallas_call(
        kernel,
        out_shape=jax.ShapeDtypeStruct((rows, outputs), jnp.bfloat16),
        grid_spec=pltpu.PrefetchScalarGridSpec(
            num_scalar_prefetch=1,
            grid=(1,),
            in_specs=[
                pl.BlockSpec((rows, half), lambda n, s: (0, s[0])),
                pl.BlockSpec((rows, half), lambda n, s: (0, 1 - s[0])),
                weight_block,
                weight_block,
                row_block,
                row_block,
                anywhere,
                anywhere,
                anywhere,
                anywhere,
            ],
            out_specs=pl.BlockSpec((rows, outputs), lambda n, s: (0, 0)),
            scratch_shapes=[
                pltpu.VMEM((2, rows, 9 * half), jnp.bfloat16),
                pltpu.VMEM((rows, outputs), jnp.bfloat16),
                pltpu.VMEM((rows, channels), jnp.bfloat16),
                pltpu.VMEM((rows, channels), jnp.bfloat16),
                pltpu.VMEM((3 * half, outputs), jnp.bfloat16),
                pltpu.VMEM((3 * half, outputs), jnp.bfloat16),
                pltpu.VMEM((2, rows, 3 * half), jnp.bfloat16),
                pltpu.SemaphoreType.DMA((4,)),
            ],
        ),
        compiler_params=pltpu.CompilerParams(dimension_semantics=("arbitrary",)),
    )(scalars, frame, frame, w_mine.reshape(9 * half, outputs), w_other.reshape(9 * half, outputs),
      gain, shift, cur, partner, t_mine.reshape(3 * half, outputs),
      t_other.reshape(3 * half, outputs))


def body(video, w_spatial, norm_gain, norm_shift, w_time):
    count, height, width, channels = video.shape
    assert count == 1 and lax.axis_size("fsdp") == 2
    pixels = height * width
    side = lax.axis_index("fsdp")
    blocks = lax.axis_size("video") * 2
    position = lax.axis_index("video") * 2 + side

    route = []
    for j in range(blocks):
        target = j + 1 if j % 2 == 1 else j - 1
        if 0 <= target < blocks and min(j, target) % CLIP != CLIP - 1:
            route.append((j, target))
    frame = video.reshape(pixels, channels)
    edge_video = lax.ppermute(frame, ("video", "fsdp"), route)
    other_spatial = swap_pair(w_spatial)
    other_time = swap_pair(w_time)

    gain = norm_gain.reshape(1, channels)
    shift = norm_shift.reshape(1, channels)
    sides = side.reshape(1).astype(jnp.int32)
    hidden = conv_norm(frame, w_spatial, other_spatial, gain, shift, sides, width)
    partner = swap_pair(hidden)
    keep_prev = (position % CLIP != 0).astype(jnp.int32)
    keep_next = (position % CLIP != CLIP - 1).astype(jnp.int32)
    keep_edge = jnp.where(side == 0, keep_prev, keep_next)
    keep_partner = jnp.where(side == 0, keep_next, keep_prev)
    scalars = jnp.stack([side.astype(jnp.int32), keep_edge, keep_partner])
    result = edge_temporal(edge_video, w_spatial, other_spatial, gain, shift, hidden, partner,
                           w_time, other_time, scalars, width)
    return result.reshape(count, height, width, channels)


def solution(mesh):
    placed = (
        P(("groups", "video", "fsdp"), None, None, None),
        P(None, None, "fsdp", None),
        P(),
        P(),
        P(None, "fsdp", None),
    )
    return jax.shard_map(
        body,
        mesh=mesh,
        in_specs=placed,
        out_specs=P(("groups", "video", "fsdp"), None, None, None),
        check_vma=False,
    )
```

```python
import functools

import jax
import jax.numpy as jnp
from jax import lax
from jax.experimental import pallas as pl
from jax.experimental.pallas import tpu as pltpu
from jax.sharding import PartitionSpec as P

GROUPS = 32
CLIP = 16
EPS = 1e-05


def swap_pair(block):
    return lax.ppermute(block, "fsdp", [(0, 1), (1, 0)])


def group_sum(row, size):
    lanes = lax.broadcasted_iota(jnp.int32, row.shape, 1)
    width = row.shape[1]
    step = 1
    while step < size:
        up = pltpu.roll(row, width - step, 1)
        down = pltpu.roll(row, step, 1)
        row = row + jnp.where((lanes & step) == 0, up, down)
        step *= 2
    return row


def build_lhs(halves, lhs_ref, width):
    rows, half = halves[0][1].shape
    col = lax.broadcasted_iota(jnp.int32, (rows, half), 0) % width
    zeros = jnp.zeros((width, half), jnp.bfloat16)
    for h, x in halves:
        xf = x.astype(jnp.float32)
        left = jnp.where(col == 0, 0.0, pltpu.roll(xf, 1, 0)).astype(jnp.bfloat16)
        right = jnp.where(col == width - 1, 0.0, pltpu.roll(xf, rows - 1, 0)).astype(jnp.bfloat16)
        for dx, v in enumerate((left, xf.astype(jnp.bfloat16), right)):
            for dy in range(3):
                lo = (dy * 3 + dx) * half
                cols = slice(lo, lo + half)
                if dy == 0:
                    lhs_ref[h, :width, cols] = zeros
                    lhs_ref[h, width:, cols] = v[: rows - width]
                elif dy == 1:
                    lhs_ref[h, :, cols] = v
                else:
                    lhs_ref[h, : rows - width, cols] = v[width:]
                    lhs_ref[h, rows - width :, cols] = zeros


def conv_norm_kernel(side_ref, xa_ref, xb_ref, wa_ref, wb_ref, gain_ref, shift_ref, o_ref,
                     lhs_ref, *, width, group):
    build_lhs(((0, xa_ref[...]), (1, xb_ref[...])), lhs_ref, width)
    dots_norm(lhs_ref, wa_ref, wb_ref, gain_ref, shift_ref, o_ref, group)


def dots_norm(lhs_ref, wa_ref, wb_ref, gain_ref, shift_ref, o_ref, group):
    rows = lhs_ref.shape[1]
    acc = jnp.dot(lhs_ref[0], wa_ref[...], preferred_element_type=jnp.float32) + jnp.dot(
        lhs_ref[1], wb_ref[...], preferred_element_type=jnp.float32
    )
    count = rows * group
    total = jnp.broadcast_to(jnp.sum(acc, axis=0, keepdims=True), (8, acc.shape[1]))
    mean = group_sum(total, group)[0:1] / count
    d = acc - mean
    spread = jnp.broadcast_to(jnp.sum(d * d, axis=0, keepdims=True), (8, acc.shape[1]))
    variance = group_sum(spread, group)[0:1] / count
    v = d * lax.rsqrt(variance + EPS) * gain_ref[...] + shift_ref[...]
    o_ref[...] = (v / (1.0 + jnp.exp(-v))).astype(o_ref.dtype)


def conv_norm(frame, w_mine, w_other, gain, shift, side, width, split=1):
    rows, channels = frame.shape
    half = w_mine.shape[2]
    outputs = w_mine.shape[3]
    group = outputs // GROUPS
    block = outputs // split
    kernel = functools.partial(conv_norm_kernel, width=width, group=group)
    weight_block = pl.BlockSpec((9 * half, block), lambda n, s: (0, n))
    row_block = pl.BlockSpec((1, block), lambda n, s: (0, n))
    return pl.pallas_call(
        kernel,
        out_shape=jax.ShapeDtypeStruct((rows, outputs), jnp.bfloat16),
        grid_spec=pltpu.PrefetchScalarGridSpec(
            num_scalar_prefetch=1,
            grid=(split,),
            in_specs=[
                pl.BlockSpec((rows, half), lambda n, s: (0, s[0])),
                pl.BlockSpec((rows, half), lambda n, s: (0, 1 - s[0])),
                weight_block,
                weight_block,
                row_block,
                row_block,
            ],
            out_specs=pl.BlockSpec((rows, block), lambda n, s: (0, n)),
            scratch_shapes=[pltpu.VMEM((2, rows, 9 * half), jnp.bfloat16)],
        ),
        compiler_params=pltpu.CompilerParams(dimension_semantics=("arbitrary",)),
    )(side, frame, frame, w_mine.reshape(9 * half, outputs), w_other.reshape(9 * half, outputs),
      gain, shift)


def edge_temporal_kernel(s_ref, x_ref, wa_ref, wb_ref, gain_ref, shift_ref,
                         cur_hbm, partner_v, wtm_hbm, wto_v, o_ref,
                         lhs_ref, edge_v, cur_v, wtm_v, tl_ref, sem,
                         *, width, group):
    copies = [
        pltpu.make_async_copy(src, dst, sem.at[i])
        for i, (src, dst) in enumerate(
            ((cur_hbm, cur_v), (wtm_hbm, wtm_v))
        )
    ]
    for copy in copies:
        copy.start()
    half = x_ref.shape[1] // 2
    build_lhs(
        [((h + s_ref[0]) % 2, x_ref[:, h * half : (h + 1) * half]) for h in range(2)], lhs_ref, width
    )
    dots_norm(lhs_ref, wa_ref, wb_ref, gain_ref, shift_ref, edge_v, group)
    for copy in copies:
        copy.wait()

    rows = x_ref.shape[0]
    keep_edge = s_ref[1] != 0
    keep_partner = s_ref[2] != 0
    for side in range(2):
        @pl.when(s_ref[0] == side)
        def _fill():
            mine = slice(side * half, (side + 1) * half)
            other = slice((1 - side) * half, (2 - side) * half)
            for h, cols in enumerate((mine, other)):
                e = edge_v[:, cols]
                p = partner_v[:, cols]
                e = jnp.where(keep_edge, e, jnp.zeros_like(e))
                p = jnp.where(keep_partner, p, jnp.zeros_like(p))
                before, after = (e, p) if side == 0 else (p, e)
                tl_ref[h, :, :half] = before
                tl_ref[h, :, half : 2 * half] = cur_v[:, cols]
                tl_ref[h, :, 2 * half :] = after

    f32 = jnp.float32
    total = jnp.dot(tl_ref[0], wtm_v[...], preferred_element_type=f32) + jnp.dot(
        tl_ref[1], wto_v[...], preferred_element_type=f32
    )
    o_ref[...] = (cur_v[...].astype(f32) + total).astype(o_ref.dtype)


def edge_temporal(frame, w_mine, w_other, gain, shift, cur, partner, t_mine, t_other, scalars,
                  width):
    rows, channels = frame.shape
    half = w_mine.shape[2]
    outputs = w_mine.shape[3]
    group = outputs // GROUPS
    kernel = functools.partial(edge_temporal_kernel, width=width, group=group)
    weight_block = pl.BlockSpec((9 * half, outputs), lambda n, s: (0, 0))
    row_block = pl.BlockSpec((1, outputs), lambda n, s: (0, 0))
    anywhere = pl.BlockSpec(memory_space=pl.ANY)
    in_vmem = pl.BlockSpec(memory_space=pltpu.VMEM)
    return pl.pallas_call(
        kernel,
        out_shape=jax.ShapeDtypeStruct((rows, outputs), jnp.bfloat16),
        grid_spec=pltpu.PrefetchScalarGridSpec(
            num_scalar_prefetch=1,
            grid=(1,),
            in_specs=[
                in_vmem,
                weight_block,
                weight_block,
                row_block,
                row_block,
                anywhere,
                in_vmem,
                anywhere,
                in_vmem,
            ],
            out_specs=pl.BlockSpec((rows, outputs), lambda n, s: (0, 0)),
            scratch_shapes=[
                pltpu.VMEM((2, rows, 9 * half), jnp.bfloat16),
                pltpu.VMEM((rows, outputs), jnp.bfloat16),
                pltpu.VMEM((rows, channels), jnp.bfloat16),
                pltpu.VMEM((3 * half, outputs), jnp.bfloat16),
                pltpu.VMEM((2, rows, 3 * half), jnp.bfloat16),
                pltpu.SemaphoreType.DMA((2,)),
            ],
        ),
        compiler_params=pltpu.CompilerParams(dimension_semantics=("arbitrary",)),
    )(scalars, frame, w_mine.reshape(9 * half, outputs), w_other.reshape(9 * half, outputs),
      gain, shift, cur, partner, t_mine.reshape(3 * half, outputs),
      t_other.reshape(3 * half, outputs))


def body(video, w_spatial, norm_gain, norm_shift, w_time):
    count, height, width, channels = video.shape
    assert count == 1 and lax.axis_size("fsdp") == 2
    pixels = height * width
    side = lax.axis_index("fsdp")
    blocks = lax.axis_size("video") * 2
    position = lax.axis_index("video") * 2 + side

    route = []
    for j in range(blocks):
        target = j + 1 if j % 2 == 1 else j - 1
        if 0 <= target < blocks and min(j, target) % CLIP != CLIP - 1:
            route.append((j, target))
    frame = video.reshape(pixels, channels)
    edge_video = lax.ppermute(frame, ("video", "fsdp"), route)
    other_spatial = swap_pair(w_spatial)
    other_time = swap_pair(w_time)

    gain = norm_gain.reshape(1, channels)
    shift = norm_shift.reshape(1, channels)
    sides = side.reshape(1).astype(jnp.int32)
    hidden = conv_norm(frame, w_spatial, other_spatial, gain, shift, sides, width)
    partner = swap_pair(hidden)
    keep_prev = (position % CLIP != 0).astype(jnp.int32)
    keep_next = (position % CLIP != CLIP - 1).astype(jnp.int32)
    keep_edge = jnp.where(side == 0, keep_prev, keep_next)
    keep_partner = jnp.where(side == 0, keep_next, keep_prev)
    scalars = jnp.stack([side.astype(jnp.int32), keep_edge, keep_partner])
    result = edge_temporal(edge_video, w_spatial, other_spatial, gain, shift, hidden, partner,
                           w_time, other_time, scalars, width)
    return result.reshape(count, height, width, channels)


def solution(mesh):
    placed = (
        P(("groups", "video", "fsdp"), None, None, None),
        P(None, None, "fsdp", None),
        P(),
        P(),
        P(None, "fsdp", None),
    )
    return jax.shard_map(
        body,
        mesh=mesh,
        in_specs=placed,
        out_specs=P(("groups", "video", "fsdp"), None, None, None),
        check_vma=False,
    )
```

```python
import functools

import jax
import jax.numpy as jnp
from jax import lax
from jax.experimental import pallas as pl
from jax.experimental.pallas import tpu as pltpu
from jax.sharding import PartitionSpec as P

GROUPS = 32
CLIP = 16
EPS = 1e-05


def swap_pair(block):
    return lax.ppermute(block, "fsdp", [(0, 1), (1, 0)])


def group_sum(row, size):
    lanes = lax.broadcasted_iota(jnp.int32, row.shape, 1)
    width = row.shape[1]
    step = 1
    while step < size:
        up = pltpu.roll(row, width - step, 1)
        down = pltpu.roll(row, step, 1)
        row = row + jnp.where((lanes & step) == 0, up, down)
        step *= 2
    return row


def conv_norm_kernel(side_ref, xa_ref, xb_ref, wa_ref, wb_ref, gain_ref, shift_ref, o_ref,
                     lhs_ref, *, width, group):
    rows, half = xa_ref.shape

    @pl.when(pl.program_id(0) == 0)
    def _prepare():
        col = lax.broadcasted_iota(jnp.int32, (rows, half), 0) % width
        zeros = jnp.zeros((width, half), jnp.bfloat16)
        for h, x_ref in enumerate((xa_ref, xb_ref)):
            xf = x_ref[...].astype(jnp.float32)
            left = jnp.where(col == 0, 0.0, pltpu.roll(xf, 1, 0)).astype(jnp.bfloat16)
            right = jnp.where(col == width - 1, 0.0, pltpu.roll(xf, rows - 1, 0)).astype(jnp.bfloat16)
            for dx, v in enumerate((left, xf.astype(jnp.bfloat16), right)):
                for dy in range(3):
                    lo = (dy * 3 + dx) * half
                    cols = slice(lo, lo + half)
                    if dy == 0:
                        lhs_ref[h, :width, cols] = zeros
                        lhs_ref[h, width:, cols] = v[: rows - width]
                    elif dy == 1:
                        lhs_ref[h, :, cols] = v
                    else:
                        lhs_ref[h, : rows - width, cols] = v[width:]
                        lhs_ref[h, rows - width :, cols] = zeros

    acc = jnp.dot(lhs_ref[0], wa_ref[...], preferred_element_type=jnp.float32) + jnp.dot(
        lhs_ref[1], wb_ref[...], preferred_element_type=jnp.float32
    )
    count = rows * group
    total = jnp.broadcast_to(jnp.sum(acc, axis=0, keepdims=True), (8, acc.shape[1]))
    mean = group_sum(total, group)[0:1] / count
    d = acc - mean
    spread = jnp.broadcast_to(jnp.sum(d * d, axis=0, keepdims=True), (8, acc.shape[1]))
    variance = group_sum(spread, group)[0:1] / count
    v = d * lax.rsqrt(variance + EPS) * gain_ref[...] + shift_ref[...]
    o_ref[...] = (v / (1.0 + jnp.exp(-v))).astype(o_ref.dtype)


def own_conv_kernel(side_ref, xa_ref, xb_ref, wa_ref, wb_ref, gain_ref, shift_ref, tm_ref, to_ref,
                    o_ref, p_ref, lhs_ref, *, width, group):
    conv_norm_kernel(side_ref, xa_ref, xb_ref, wa_ref, wb_ref, gain_ref, shift_ref, o_ref,
                     lhs_ref, width=width, group=group)
    half = xa_ref.shape[1]
    for side in range(2):
        @pl.when(side_ref[0] == side)
        def _tap():
            mine = slice(side * half, (side + 1) * half)
            other = slice((1 - side) * half, (2 - side) * half)
            p_ref[...] = jnp.dot(o_ref[:, mine], tm_ref[0], preferred_element_type=jnp.float32) + jnp.dot(
                o_ref[:, other], to_ref[0], preferred_element_type=jnp.float32
            )


def own_conv(frame, w_mine, w_other, gain, shift, t_mine, t_other, side, width):
    rows, channels = frame.shape
    half = w_mine.shape[2]
    outputs = w_mine.shape[3]
    group = outputs // GROUPS
    kernel = functools.partial(own_conv_kernel, width=width, group=group)
    weight_block = pl.BlockSpec((9 * half, outputs), lambda n, s: (0, 0))
    row_block = pl.BlockSpec((1, outputs), lambda n, s: (0, 0))
    tap_block = pl.BlockSpec((1, half, outputs), lambda n, s: (1, 0, 0))
    whole = pl.BlockSpec((rows, outputs), lambda n, s: (0, 0))
    return pl.pallas_call(
        kernel,
        out_shape=(
            jax.ShapeDtypeStruct((rows, outputs), jnp.bfloat16),
            jax.ShapeDtypeStruct((rows, outputs), jnp.float32),
        ),
        grid_spec=pltpu.PrefetchScalarGridSpec(
            num_scalar_prefetch=1,
            grid=(1,),
            in_specs=[
                pl.BlockSpec((rows, half), lambda n, s: (0, s[0])),
                pl.BlockSpec((rows, half), lambda n, s: (0, 1 - s[0])),
                weight_block,
                weight_block,
                row_block,
                row_block,
                tap_block,
                tap_block,
            ],
            out_specs=(whole, whole),
            scratch_shapes=[pltpu.VMEM((2, rows, 9 * half), jnp.bfloat16)],
        ),
    )(side, frame, frame, w_mine.reshape(9 * half, outputs), w_other.reshape(9 * half, outputs),
      gain, shift, t_mine, t_other)


def conv_norm(frame, w_mine, w_other, gain, shift, side, width, split=1):
    rows, channels = frame.shape
    half = w_mine.shape[2]
    outputs = w_mine.shape[3]
    group = outputs // GROUPS
    block = outputs // split
    kernel = functools.partial(conv_norm_kernel, width=width, group=group)
    weight_block = pl.BlockSpec((9 * half, block), lambda n, s: (0, n))
    row_block = pl.BlockSpec((1, block), lambda n, s: (0, n))
    return pl.pallas_call(
        kernel,
        out_shape=jax.ShapeDtypeStruct((rows, outputs), jnp.bfloat16),
        grid_spec=pltpu.PrefetchScalarGridSpec(
            num_scalar_prefetch=1,
            grid=(split,),
            in_specs=[
                pl.BlockSpec((rows, half), lambda n, s: (0, s[0])),
                pl.BlockSpec((rows, half), lambda n, s: (0, 1 - s[0])),
                weight_block,
                weight_block,
                row_block,
                row_block,
            ],
            out_specs=pl.BlockSpec((rows, block), lambda n, s: (0, n)),
            scratch_shapes=[pltpu.VMEM((2, rows, 9 * half), jnp.bfloat16)],
        ),
        compiler_params=pltpu.CompilerParams(dimension_semantics=("arbitrary",)),
    )(side, frame, frame, w_mine.reshape(9 * half, outputs), w_other.reshape(9 * half, outputs),
      gain, shift)


def edge_temporal_kernel(s_ref, xa_ref, xb_ref, wa_ref, wb_ref, gain_ref, shift_ref,
                         cur_hbm, own_hbm, partner_hbm, wtm_hbm, wto_hbm, o_ref,
                         lhs_ref, edge_v, cur_v, own_v, partner_v, wtm_v, wto_v, tl_ref, sem,
                         *, width, group):
    copies = [
        pltpu.make_async_copy(src, dst, sem.at[i])
        for i, (src, dst) in enumerate(
            ((cur_hbm, cur_v), (own_hbm, own_v), (partner_hbm, partner_v),
             (wtm_hbm.at[0], wtm_v.at[0]), (wtm_hbm.at[2], wtm_v.at[1]),
             (wto_hbm.at[0], wto_v.at[0]), (wto_hbm.at[2], wto_v.at[1]))
        )
    ]
    for copy in copies:
        copy.start()
    conv_norm_kernel(s_ref, xa_ref, xb_ref, wa_ref, wb_ref, gain_ref, shift_ref, edge_v,
                     lhs_ref, width=width, group=group)
    for copy in copies:
        copy.wait()

    rows, half = xa_ref.shape
    keep_edge = s_ref[1] != 0
    keep_partner = s_ref[2] != 0
    for side in range(2):
        @pl.when(s_ref[0] == side)
        def _fill():
            mine = slice(side * half, (side + 1) * half)
            other = slice((1 - side) * half, (2 - side) * half)
            for h, cols in enumerate((mine, other)):
                e = edge_v[:, cols]
                p = partner_v[:, cols]
                e = jnp.where(keep_edge, e, jnp.zeros_like(e))
                p = jnp.where(keep_partner, p, jnp.zeros_like(p))
                before, after = (e, p) if side == 0 else (p, e)
                tl_ref[h, :, :half] = before
                tl_ref[h, :, half:] = after

    f32 = jnp.float32
    taps = wtm_v.shape[0] * wtm_v.shape[1]
    total = jnp.dot(tl_ref[0], wtm_v[...].reshape(taps, -1), preferred_element_type=f32) + jnp.dot(
        tl_ref[1], wto_v[...].reshape(taps, -1), preferred_element_type=f32
    )
    total = total + own_v[...]
    o_ref[...] = (cur_v[...].astype(f32) + total).astype(o_ref.dtype)


def edge_temporal(frame, w_mine, w_other, gain, shift, cur, own, partner, t_mine, t_other,
                  scalars, width):
    rows, channels = frame.shape
    half = w_mine.shape[2]
    outputs = w_mine.shape[3]
    group = outputs // GROUPS
    kernel = functools.partial(edge_temporal_kernel, width=width, group=group)
    weight_block = pl.BlockSpec((9 * half, outputs), lambda n, s: (0, 0))
    row_block = pl.BlockSpec((1, outputs), lambda n, s: (0, 0))
    anywhere = pl.BlockSpec(memory_space=pl.ANY)
    return pl.pallas_call(
        kernel,
        out_shape=jax.ShapeDtypeStruct((rows, outputs), jnp.bfloat16),
        grid_spec=pltpu.PrefetchScalarGridSpec(
            num_scalar_prefetch=1,
            grid=(1,),
            in_specs=[
                pl.BlockSpec((rows, half), lambda n, s: (0, s[0])),
                pl.BlockSpec((rows, half), lambda n, s: (0, 1 - s[0])),
                weight_block,
                weight_block,
                row_block,
                row_block,
                anywhere,
                anywhere,
                anywhere,
                anywhere,
                anywhere,
            ],
            out_specs=pl.BlockSpec((rows, outputs), lambda n, s: (0, 0)),
            scratch_shapes=[
                pltpu.VMEM((2, rows, 9 * half), jnp.bfloat16),
                pltpu.VMEM((rows, outputs), jnp.bfloat16),
                pltpu.VMEM((rows, channels), jnp.bfloat16),
                pltpu.VMEM((rows, outputs), jnp.float32),
                pltpu.VMEM((rows, channels), jnp.bfloat16),
                pltpu.VMEM((2, half, outputs), jnp.bfloat16),
                pltpu.VMEM((2, half, outputs), jnp.bfloat16),
                pltpu.VMEM((2, rows, 2 * half), jnp.bfloat16),
                pltpu.SemaphoreType.DMA((7,)),
            ],
        ),
        compiler_params=pltpu.CompilerParams(dimension_semantics=("arbitrary",)),
    )(scalars, frame, frame, w_mine.reshape(9 * half, outputs), w_other.reshape(9 * half, outputs),
      gain, shift, cur, own, partner, t_mine, t_other)


def body(video, w_spatial, norm_gain, norm_shift, w_time):
    count, height, width, channels = video.shape
    assert count == 1 and lax.axis_size("fsdp") == 2
    pixels = height * width
    side = lax.axis_index("fsdp")
    blocks = lax.axis_size("video") * 2
    position = lax.axis_index("video") * 2 + side

    route = []
    for j in range(blocks):
        target = j + 1 if j % 2 == 1 else j - 1
        if 0 <= target < blocks and min(j, target) % CLIP != CLIP - 1:
            route.append((j, target))
    frame = video.reshape(pixels, channels)
    edge_video = lax.ppermute(frame, ("video", "fsdp"), route)
    other_spatial = swap_pair(w_spatial)
    other_time = swap_pair(w_time)

    gain = norm_gain.reshape(1, channels)
    shift = norm_shift.reshape(1, channels)
    sides = side.reshape(1).astype(jnp.int32)
    hidden, own_tap = own_conv(frame, w_spatial, other_spatial, gain, shift, w_time, other_time,
                               sides, width)
    partner = swap_pair(hidden)
    keep_prev = (position % CLIP != 0).astype(jnp.int32)
    keep_next = (position % CLIP != CLIP - 1).astype(jnp.int32)
    keep_edge = jnp.where(side == 0, keep_prev, keep_next)
    keep_partner = jnp.where(side == 0, keep_next, keep_prev)
    scalars = jnp.stack([side.astype(jnp.int32), keep_edge, keep_partner])
    result = edge_temporal(edge_video, w_spatial, other_spatial, gain, shift, hidden, own_tap,
                           partner, w_time, other_time, scalars, width)
    return result.reshape(count, height, width, channels)


def solution(mesh):
    placed = (
        P(("groups", "video", "fsdp"), None, None, None),
        P(None, None, "fsdp", None),
        P(),
        P(),
        P(None, "fsdp", None),
    )
    return jax.shard_map(
        body,
        mesh=mesh,
        in_specs=placed,
        out_specs=P(("groups", "video", "fsdp"), None, None, None),
        check_vma=False,
    )
```

```python
import functools

import jax
import jax.numpy as jnp
from jax import lax
from jax.experimental import pallas as pl
from jax.experimental.pallas import tpu as pltpu
from jax.sharding import PartitionSpec as P

GROUPS = 32
CLIP = 16
EPS = 1e-05


def swap_pair(block):
    return lax.ppermute(block, "fsdp", [(0, 1), (1, 0)])


def group_sum(row, size):
    lanes = lax.broadcasted_iota(jnp.int32, row.shape, 1)
    width = row.shape[1]
    step = 1
    while step < size:
        up = pltpu.roll(row, width - step, 1)
        down = pltpu.roll(row, step, 1)
        row = row + jnp.where((lanes & step) == 0, up, down)
        step *= 2
    return row


def build_lhs(halves, lhs_ref, width):
    rows, half = halves[0][1].shape
    col = lax.broadcasted_iota(jnp.int32, (rows, half), 0) % width
    zeros = jnp.zeros((width, half), jnp.bfloat16)
    for h, x in halves:
        xf = x.astype(jnp.float32)
        left = jnp.where(col == 0, 0.0, pltpu.roll(xf, 1, 0)).astype(jnp.bfloat16)
        right = jnp.where(col == width - 1, 0.0, pltpu.roll(xf, rows - 1, 0)).astype(jnp.bfloat16)
        for dx, v in enumerate((left, xf.astype(jnp.bfloat16), right)):
            for dy in range(3):
                lo = (dy * 3 + dx) * half
                cols = slice(lo, lo + half)
                if dy == 0:
                    lhs_ref[h, :width, cols] = zeros
                    lhs_ref[h, width:, cols] = v[: rows - width]
                elif dy == 1:
                    lhs_ref[h, :, cols] = v
                else:
                    lhs_ref[h, : rows - width, cols] = v[width:]
                    lhs_ref[h, rows - width :, cols] = zeros


def norm_silu(acc, gain_ref, shift_ref, o_ref, rows, group):
    count = rows * group
    total = jnp.broadcast_to(jnp.sum(acc, axis=0, keepdims=True), (8, acc.shape[1]))
    mean = group_sum(total, group)[0:1] / count
    d = acc - mean
    spread = jnp.broadcast_to(jnp.sum(d * d, axis=0, keepdims=True), (8, acc.shape[1]))
    variance = group_sum(spread, group)[0:1] / count
    v = d * lax.rsqrt(variance + EPS) * gain_ref[...] + shift_ref[...]
    o_ref[...] = (v / (1.0 + jnp.exp(-v))).astype(o_ref.dtype)


def conv_norm_kernel(side_ref, xa_ref, xb_ref, wa_ref, wb_ref, gain_ref, shift_ref, o_ref,
                     lhs_ref, *, width, group):
    rows = xa_ref.shape[0]

    @pl.when(pl.program_id(0) == 0)
    def _prepare():
        build_lhs(((0, xa_ref[...]), (1, xb_ref[...])), lhs_ref, width)

    acc = jnp.dot(lhs_ref[0], wa_ref[...], preferred_element_type=jnp.float32) + jnp.dot(
        lhs_ref[1], wb_ref[...], preferred_element_type=jnp.float32
    )
    norm_silu(acc, gain_ref, shift_ref, o_ref, rows, group)


def conv_norm(frame, w_mine, w_other, gain, shift, side, width, split=1):
    rows, channels = frame.shape
    half = w_mine.shape[2]
    outputs = w_mine.shape[3]
    group = outputs // GROUPS
    block = outputs // split
    kernel = functools.partial(conv_norm_kernel, width=width, group=group)
    weight_block = pl.BlockSpec((9 * half, block), lambda n, s: (0, n))
    row_block = pl.BlockSpec((1, block), lambda n, s: (0, n))
    return pl.pallas_call(
        kernel,
        out_shape=jax.ShapeDtypeStruct((rows, outputs), jnp.bfloat16),
        grid_spec=pltpu.PrefetchScalarGridSpec(
            num_scalar_prefetch=1,
            grid=(split,),
            in_specs=[
                pl.BlockSpec((rows, half), lambda n, s: (0, s[0])),
                pl.BlockSpec((rows, half), lambda n, s: (0, 1 - s[0])),
                weight_block,
                weight_block,
                row_block,
                row_block,
            ],
            out_specs=pl.BlockSpec((rows, block), lambda n, s: (0, n)),
            scratch_shapes=[pltpu.VMEM((2, rows, 9 * half), jnp.bfloat16)],
        ),
        compiler_params=pltpu.CompilerParams(dimension_semantics=("arbitrary",)),
    )(side, frame, frame, w_mine.reshape(9 * half, outputs), w_other.reshape(9 * half, outputs),
      gain, shift)


def edge_temporal_kernel(s_ref, xa_ref, xb_ref, wa_hbm, wb_hbm, gain_ref, shift_ref,
                         cur_hbm, partner_hbm, wtm_hbm, wto_hbm, o_ref,
                         lhs_ref, wa_v, wb_v, edge_v, cur_v, partner_v, wtm_v, wto_v, tl_ref, sem,
                         wsem, *, width, group, chunks=2):
    copies = [
        pltpu.make_async_copy(src, dst, sem.at[i])
        for i, (src, dst) in enumerate(
            ((cur_hbm, cur_v), (partner_hbm, partner_v), (wtm_hbm, wtm_v), (wto_hbm, wto_v))
        )
    ]
    size = wa_hbm.shape[0] // chunks
    weight_copies = [
        [
            pltpu.make_async_copy(w_hbm.at[pl.ds(k * size, size)], w_v.at[pl.ds(k * size, size)],
                                  wsem.at[2 * k + i])
            for i, (w_hbm, w_v) in enumerate(((wa_hbm, wa_v), (wb_hbm, wb_v)))
        ]
        for k in range(chunks)
    ]
    for pair in weight_copies:
        for copy in pair:
            copy.start()
    for copy in copies:
        copy.start()
    rows = xa_ref.shape[0]

    @pl.when(pl.program_id(0) == 0)
    def _prepare():
        build_lhs(((0, xa_ref[...]), (1, xb_ref[...])), lhs_ref, width)

    acc = None
    for k, pair in enumerate(weight_copies):
        for copy in pair:
            copy.wait()
        cols = pl.ds(k * size, size)
        term = jnp.dot(lhs_ref[0, :, cols], wa_v[cols, :], preferred_element_type=jnp.float32) + jnp.dot(
            lhs_ref[1, :, cols], wb_v[cols, :], preferred_element_type=jnp.float32
        )
        acc = term if acc is None else acc + term
    norm_silu(acc, gain_ref, shift_ref, edge_v, rows, group)
    for copy in copies:
        copy.wait()

    rows, half = xa_ref.shape
    keep_edge = s_ref[1] != 0
    keep_partner = s_ref[2] != 0
    for side in range(2):
        @pl.when(s_ref[0] == side)
        def _fill():
            mine = slice(side * half, (side + 1) * half)
            other = slice((1 - side) * half, (2 - side) * half)
            for h, cols in enumerate((mine, other)):
                e = edge_v[:, cols]
                p = partner_v[:, cols]
                e = jnp.where(keep_edge, e, jnp.zeros_like(e))
                p = jnp.where(keep_partner, p, jnp.zeros_like(p))
                before, after = (e, p) if side == 0 else (p, e)
                tl_ref[h, :, :half] = before
                tl_ref[h, :, half : 2 * half] = cur_v[:, cols]
                tl_ref[h, :, 2 * half :] = after

    f32 = jnp.float32
    total = jnp.dot(tl_ref[0], wtm_v[...], preferred_element_type=f32) + jnp.dot(
        tl_ref[1], wto_v[...], preferred_element_type=f32
    )
    o_ref[...] = (cur_v[...].astype(f32) + total).astype(o_ref.dtype)


def edge_temporal(frame, w_mine, w_other, gain, shift, cur, partner, t_mine, t_other, scalars,
                  width):
    rows, channels = frame.shape
    half = w_mine.shape[2]
    outputs = w_mine.shape[3]
    group = outputs // GROUPS
    kernel = functools.partial(edge_temporal_kernel, width=width, group=group)
    weight_block = pl.BlockSpec((9 * half, outputs), lambda n, s: (0, 0))
    row_block = pl.BlockSpec((1, outputs), lambda n, s: (0, 0))
    anywhere = pl.BlockSpec(memory_space=pl.ANY)
    return pl.pallas_call(
        kernel,
        out_shape=jax.ShapeDtypeStruct((rows, outputs), jnp.bfloat16),
        grid_spec=pltpu.PrefetchScalarGridSpec(
            num_scalar_prefetch=1,
            grid=(1,),
            in_specs=[
                pl.BlockSpec((rows, half), lambda n, s: (0, s[0])),
                pl.BlockSpec((rows, half), lambda n, s: (0, 1 - s[0])),
                anywhere,
                anywhere,
                row_block,
                row_block,
                anywhere,
                anywhere,
                anywhere,
                anywhere,
            ],
            out_specs=pl.BlockSpec((rows, outputs), lambda n, s: (0, 0)),
            scratch_shapes=[
                pltpu.VMEM((2, rows, 9 * half), jnp.bfloat16),
                pltpu.VMEM((9 * half, outputs), jnp.bfloat16),
                pltpu.VMEM((9 * half, outputs), jnp.bfloat16),
                pltpu.VMEM((rows, outputs), jnp.bfloat16),
                pltpu.VMEM((rows, channels), jnp.bfloat16),
                pltpu.VMEM((rows, channels), jnp.bfloat16),
                pltpu.VMEM((3 * half, outputs), jnp.bfloat16),
                pltpu.VMEM((3 * half, outputs), jnp.bfloat16),
                pltpu.VMEM((2, rows, 3 * half), jnp.bfloat16),
                pltpu.SemaphoreType.DMA((4,)),
                pltpu.SemaphoreType.DMA((4,)),
            ],
        ),
        compiler_params=pltpu.CompilerParams(dimension_semantics=("arbitrary",)),
    )(scalars, frame, frame, w_mine.reshape(9 * half, outputs), w_other.reshape(9 * half, outputs),
      gain, shift, cur, partner, t_mine.reshape(3 * half, outputs),
      t_other.reshape(3 * half, outputs))


def body(video, w_spatial, norm_gain, norm_shift, w_time):
    count, height, width, channels = video.shape
    assert count == 1 and lax.axis_size("fsdp") == 2
    pixels = height * width
    side = lax.axis_index("fsdp")
    blocks = lax.axis_size("video") * 2
    position = lax.axis_index("video") * 2 + side

    route = []
    for j in range(blocks):
        target = j + 1 if j % 2 == 1 else j - 1
        if 0 <= target < blocks and min(j, target) % CLIP != CLIP - 1:
            route.append((j, target))
    frame = video.reshape(pixels, channels)
    edge_video = lax.ppermute(frame, ("video", "fsdp"), route)
    other_spatial = swap_pair(w_spatial)
    other_time = swap_pair(w_time)

    gain = norm_gain.reshape(1, channels)
    shift = norm_shift.reshape(1, channels)
    sides = side.reshape(1).astype(jnp.int32)
    hidden = conv_norm(frame, w_spatial, other_spatial, gain, shift, sides, width)
    partner = swap_pair(hidden)
    keep_prev = (position % CLIP != 0).astype(jnp.int32)
    keep_next = (position % CLIP != CLIP - 1).astype(jnp.int32)
    keep_edge = jnp.where(side == 0, keep_prev, keep_next)
    keep_partner = jnp.where(side == 0, keep_next, keep_prev)
    scalars = jnp.stack([side.astype(jnp.int32), keep_edge, keep_partner])
    result = edge_temporal(edge_video, w_spatial, other_spatial, gain, shift, hidden, partner,
                           w_time, other_time, scalars, width)
    return result.reshape(count, height, width, channels)


def solution(mesh):
    placed = (
        P(("groups", "video", "fsdp"), None, None, None),
        P(None, None, "fsdp", None),
        P(),
        P(),
        P(None, "fsdp", None),
    )
    return jax.shard_map(
        body,
        mesh=mesh,
        in_specs=placed,
        out_specs=P(("groups", "video", "fsdp"), None, None, None),
        check_vma=False,
    )
```

```python
import functools

import jax
import jax.numpy as jnp
from jax import lax
from jax.experimental import pallas as pl
from jax.experimental.pallas import tpu as pltpu
from jax.sharding import PartitionSpec as P

GROUPS = 32
CLIP = 16
EPS = 1e-05


def swap_pair(block):
    return lax.ppermute(block, "fsdp", [(0, 1), (1, 0)])


def group_sum(row, size):
    lanes = lax.broadcasted_iota(jnp.int32, row.shape, 1)
    width = row.shape[1]
    step = 1
    while step < size:
        up = pltpu.roll(row, width - step, 1)
        down = pltpu.roll(row, step, 1)
        row = row + jnp.where((lanes & step) == 0, up, down)
        step *= 2
    return row


def conv_norm_kernel(side_ref, xa_ref, xb_ref, wa_ref, wb_ref, gain_ref, shift_ref, o_ref,
                     lhs_ref, *, width, group):
    rows, half = xa_ref.shape

    @pl.when(pl.program_id(0) == 0)
    def _prepare():
        col = lax.broadcasted_iota(jnp.int32, (rows, half), 0) % width
        zeros = jnp.zeros((width, half), jnp.bfloat16)
        for h, x_ref in enumerate((xa_ref, xb_ref)):
            xf = x_ref[...].astype(jnp.float32)
            left = jnp.where(col == 0, 0.0, pltpu.roll(xf, 1, 0)).astype(jnp.bfloat16)
            right = jnp.where(col == width - 1, 0.0, pltpu.roll(xf, rows - 1, 0)).astype(jnp.bfloat16)
            for dx, v in enumerate((left, xf.astype(jnp.bfloat16), right)):
                for dy in range(3):
                    lo = (dy * 3 + dx) * half
                    cols = slice(lo, lo + half)
                    if dy == 0:
                        lhs_ref[h, :width, cols] = zeros
                        lhs_ref[h, width:, cols] = v[: rows - width]
                    elif dy == 1:
                        lhs_ref[h, :, cols] = v
                    else:
                        lhs_ref[h, : rows - width, cols] = v[width:]
                        lhs_ref[h, rows - width :, cols] = zeros

    acc = jnp.dot(lhs_ref[0], wa_ref[...], preferred_element_type=jnp.float32) + jnp.dot(
        lhs_ref[1], wb_ref[...], preferred_element_type=jnp.float32
    )
    count = rows * group
    total = jnp.broadcast_to(jnp.sum(acc, axis=0, keepdims=True), (8, acc.shape[1]))
    mean = group_sum(total, group)[0:1] / count
    d = acc - mean
    spread = jnp.broadcast_to(jnp.sum(d * d, axis=0, keepdims=True), (8, acc.shape[1]))
    variance = group_sum(spread, group)[0:1] / count
    v = d * lax.rsqrt(variance + EPS) * gain_ref[...] + shift_ref[...]
    o_ref[...] = (v / (1.0 + jnp.exp(-v))).astype(o_ref.dtype)


def conv_norm(frame, w_mine, w_other, gain, shift, side, width, split=1):
    rows, channels = frame.shape
    half = w_mine.shape[2]
    outputs = w_mine.shape[3]
    group = outputs // GROUPS
    block = outputs // split
    kernel = functools.partial(conv_norm_kernel, width=width, group=group)
    weight_block = pl.BlockSpec((9 * half, block), lambda n, s: (0, n))
    row_block = pl.BlockSpec((1, block), lambda n, s: (0, n))
    return pl.pallas_call(
        kernel,
        out_shape=jax.ShapeDtypeStruct((rows, outputs), jnp.bfloat16),
        grid_spec=pltpu.PrefetchScalarGridSpec(
            num_scalar_prefetch=1,
            grid=(split,),
            in_specs=[
                pl.BlockSpec((rows, half), lambda n, s: (0, s[0])),
                pl.BlockSpec((rows, half), lambda n, s: (0, 1 - s[0])),
                weight_block,
                weight_block,
                row_block,
                row_block,
            ],
            out_specs=pl.BlockSpec((rows, block), lambda n, s: (0, n)),
            scratch_shapes=[pltpu.VMEM((2, rows, 9 * half), jnp.bfloat16)],
        ),
        compiler_params=pltpu.CompilerParams(dimension_semantics=("arbitrary",)),
    )(side, frame, frame, w_mine.reshape(9 * half, outputs), w_other.reshape(9 * half, outputs),
      gain, shift)


def edge_temporal_kernel(s_ref, xa_ref, xb_ref, wa_ref, wb_ref, gain_ref, shift_ref,
                         cur_hbm, partner_hbm, wtm_hbm, wto_hbm, o_ref,
                         lhs_ref, edge_v, cur_v, partner_v, wt_v, sem, *, width, group):
    side = s_ref[0]
    half = wtm_hbm.shape[1]
    edge_tap = 2 * side
    taps = (edge_tap, 1, 2 - edge_tap)
    copies = [
        pltpu.make_async_copy(cur_hbm, cur_v, sem.at[0]),
        pltpu.make_async_copy(partner_hbm, partner_v, sem.at[1]),
    ]
    for slot, tap in enumerate(taps):
        copies.append(pltpu.make_async_copy(
            wtm_hbm.at[tap], wt_v.at[slot, pl.ds(side * half, half)], sem.at[2 + 2 * slot]))
        copies.append(pltpu.make_async_copy(
            wto_hbm.at[tap], wt_v.at[slot, pl.ds((1 - side) * half, half)], sem.at[3 + 2 * slot]))
    for copy in copies:
        copy.start()
    conv_norm_kernel(s_ref, xa_ref, xb_ref, wa_ref, wb_ref, gain_ref, shift_ref, edge_v,
                     lhs_ref, width=width, group=group)
    for copy in copies:
        copy.wait()

    f32 = jnp.float32
    keep_edge = s_ref[1].astype(f32)
    keep_partner = s_ref[2].astype(f32)
    own = jnp.dot(cur_v[...], wt_v[1], preferred_element_type=f32)
    edge = jnp.dot(edge_v[...], wt_v[0], preferred_element_type=f32)
    partner = jnp.dot(partner_v[...], wt_v[2], preferred_element_type=f32)
    total = own + keep_edge * edge + keep_partner * partner
    o_ref[...] = (cur_v[...].astype(f32) + total).astype(o_ref.dtype)


def edge_temporal(frame, w_mine, w_other, gain, shift, cur, partner, t_mine, t_other, scalars,
                  width):
    rows, channels = frame.shape
    half = w_mine.shape[2]
    outputs = w_mine.shape[3]
    group = outputs // GROUPS
    kernel = functools.partial(edge_temporal_kernel, width=width, group=group)
    weight_block = pl.BlockSpec((9 * half, outputs), lambda n, s: (0, 0))
    row_block = pl.BlockSpec((1, outputs), lambda n, s: (0, 0))
    anywhere = pl.BlockSpec(memory_space=pl.ANY)
    return pl.pallas_call(
        kernel,
        out_shape=jax.ShapeDtypeStruct((rows, outputs), jnp.bfloat16),
        grid_spec=pltpu.PrefetchScalarGridSpec(
            num_scalar_prefetch=1,
            grid=(1,),
            in_specs=[
                pl.BlockSpec((rows, half), lambda n, s: (0, s[0])),
                pl.BlockSpec((rows, half), lambda n, s: (0, 1 - s[0])),
                weight_block,
                weight_block,
                row_block,
                row_block,
                anywhere,
                anywhere,
                anywhere,
                anywhere,
            ],
            out_specs=pl.BlockSpec((rows, outputs), lambda n, s: (0, 0)),
            scratch_shapes=[
                pltpu.VMEM((2, rows, 9 * half), jnp.bfloat16),
                pltpu.VMEM((rows, outputs), jnp.bfloat16),
                pltpu.VMEM((rows, channels), jnp.bfloat16),
                pltpu.VMEM((rows, channels), jnp.bfloat16),
                pltpu.VMEM((3, channels, outputs), jnp.bfloat16),
                pltpu.SemaphoreType.DMA((8,)),
            ],
        ),
        compiler_params=pltpu.CompilerParams(dimension_semantics=("arbitrary",)),
    )(scalars, frame, frame, w_mine.reshape(9 * half, outputs), w_other.reshape(9 * half, outputs),
      gain, shift, cur, partner, t_mine, t_other)


def body(video, w_spatial, norm_gain, norm_shift, w_time):
    count, height, width, channels = video.shape
    assert count == 1 and lax.axis_size("fsdp") == 2
    pixels = height * width
    side = lax.axis_index("fsdp")
    blocks = lax.axis_size("video") * 2
    position = lax.axis_index("video") * 2 + side

    route = []
    for j in range(blocks):
        target = j + 1 if j % 2 == 1 else j - 1
        if 0 <= target < blocks and min(j, target) % CLIP != CLIP - 1:
            route.append((j, target))
    frame = video.reshape(pixels, channels)
    edge_video = lax.ppermute(frame, ("video", "fsdp"), route)
    other_spatial = swap_pair(w_spatial)
    other_time = swap_pair(w_time)

    gain = norm_gain.reshape(1, channels)
    shift = norm_shift.reshape(1, channels)
    sides = side.reshape(1).astype(jnp.int32)
    hidden = conv_norm(frame, w_spatial, other_spatial, gain, shift, sides, width)
    partner = swap_pair(hidden)
    keep_prev = (position % CLIP != 0).astype(jnp.int32)
    keep_next = (position % CLIP != CLIP - 1).astype(jnp.int32)
    keep_edge = jnp.where(side == 0, keep_prev, keep_next)
    keep_partner = jnp.where(side == 0, keep_next, keep_prev)
    scalars = jnp.stack([side.astype(jnp.int32), keep_edge, keep_partner])
    result = edge_temporal(edge_video, w_spatial, other_spatial, gain, shift, hidden, partner,
                           w_time, other_time, scalars, width)
    return result.reshape(count, height, width, channels)


def solution(mesh):
    placed = (
        P(("groups", "video", "fsdp"), None, None, None),
        P(None, None, "fsdp", None),
        P(),
        P(),
        P(None, "fsdp", None),
    )
    return jax.shard_map(
        body,
        mesh=mesh,
        in_specs=placed,
        out_specs=P(("groups", "video", "fsdp"), None, None, None),
        check_vma=False,
    )
```

```python
import functools

import jax
import jax.numpy as jnp
from jax import lax
from jax.experimental import pallas as pl
from jax.experimental.pallas import tpu as pltpu
from jax.sharding import PartitionSpec as P

GROUPS = 32
CLIP = 16
EPS = 1e-05


def swap_pair(block):
    return lax.ppermute(block, "fsdp", [(0, 1), (1, 0)])


def group_sum(row, size):
    lanes = lax.broadcasted_iota(jnp.int32, row.shape, 1)
    width = row.shape[1]
    step = 1
    while step < size:
        up = pltpu.roll(row, width - step, 1)
        down = pltpu.roll(row, step, 1)
        row = row + jnp.where((lanes & step) == 0, up, down)
        step *= 2
    return row


def conv_norm_kernel(side_ref, xa_ref, xb_ref, wa_ref, wb_ref, gain_ref, shift_ref, o_ref,
                     lhs_ref, *, width, group):
    rows, half = xa_ref.shape

    @pl.when(pl.program_id(0) == 0)
    def _prepare():
        col = lax.broadcasted_iota(jnp.int32, (rows, half), 0) % width
        zeros = jnp.zeros((width, half), jnp.bfloat16)
        for h, x_ref in enumerate((xa_ref, xb_ref)):
            xf = x_ref[...].astype(jnp.float32)
            left = jnp.where(col == 0, 0.0, pltpu.roll(xf, 1, 0)).astype(jnp.bfloat16)
            right = jnp.where(col == width - 1, 0.0, pltpu.roll(xf, rows - 1, 0)).astype(jnp.bfloat16)
            for dx, v in enumerate((left, xf.astype(jnp.bfloat16), right)):
                for dy in range(3):
                    lo = (dy * 3 + dx) * half
                    cols = slice(lo, lo + half)
                    if dy == 0:
                        lhs_ref[h, :width, cols] = zeros
                        lhs_ref[h, width:, cols] = v[: rows - width]
                    elif dy == 1:
                        lhs_ref[h, :, cols] = v
                    else:
                        lhs_ref[h, : rows - width, cols] = v[width:]
                        lhs_ref[h, rows - width :, cols] = zeros

    acc = jnp.dot(lhs_ref[0], wa_ref[...], preferred_element_type=jnp.float32) + jnp.dot(
        lhs_ref[1], wb_ref[...], preferred_element_type=jnp.float32
    )
    count = rows * group
    total = jnp.broadcast_to(jnp.sum(acc, axis=0, keepdims=True), (8, acc.shape[1]))
    mean = group_sum(total, group)[0:1] / count
    d = acc - mean
    spread = jnp.broadcast_to(jnp.sum(d * d, axis=0, keepdims=True), (8, acc.shape[1]))
    variance = group_sum(spread, group)[0:1] / count
    v = d * lax.rsqrt(variance + EPS) * gain_ref[...] + shift_ref[...]
    o_ref[...] = (v / (1.0 + jnp.exp(-v))).astype(o_ref.dtype)


def conv_norm(frame, w_mine, w_other, gain, shift, side, width, split=1):
    rows, channels = frame.shape
    half = w_mine.shape[2]
    outputs = w_mine.shape[3]
    group = outputs // GROUPS
    block = outputs // split
    kernel = functools.partial(conv_norm_kernel, width=width, group=group)
    weight_block = pl.BlockSpec((9 * half, block), lambda n, s: (0, n))
    row_block = pl.BlockSpec((1, block), lambda n, s: (0, n))
    return pl.pallas_call(
        kernel,
        out_shape=jax.ShapeDtypeStruct((rows, outputs), jnp.bfloat16),
        grid_spec=pltpu.PrefetchScalarGridSpec(
            num_scalar_prefetch=1,
            grid=(split,),
            in_specs=[
                pl.BlockSpec((rows, half), lambda n, s: (0, s[0])),
                pl.BlockSpec((rows, half), lambda n, s: (0, 1 - s[0])),
                weight_block,
                weight_block,
                row_block,
                row_block,
            ],
            out_specs=pl.BlockSpec((rows, block), lambda n, s: (0, n)),
            scratch_shapes=[pltpu.VMEM((2, rows, 9 * half), jnp.bfloat16)],
        ),
        compiler_params=pltpu.CompilerParams(dimension_semantics=("arbitrary",)),
    )(side, frame, frame, w_mine.reshape(9 * half, outputs), w_other.reshape(9 * half, outputs),
      gain, shift)


def edge_temporal_kernel(s_ref, xa_ref, xb_ref, wa_ref, wb_ref, gain_ref, shift_ref,
                         cur_hbm, partner_hbm, wtm_hbm, wto_hbm, o_ref,
                         lhs_ref, edge_v, cur_v, partner_v, wtm_v, wto_v, tl_ref, sem,
                         *, width, group):
    copies = [
        pltpu.make_async_copy(src, dst, sem.at[i])
        for i, (src, dst) in enumerate(
            ((cur_hbm, cur_v), (partner_hbm, partner_v), (wtm_hbm, wtm_v), (wto_hbm, wto_v))
        )
    ]
    conv_norm_kernel(s_ref, xa_ref, xb_ref, wa_ref, wb_ref, gain_ref, shift_ref, edge_v,
                     lhs_ref, width=width, group=group)
    for copy in copies:
        copy.start()
    for copy in copies:
        copy.wait()

    rows, half = xa_ref.shape
    keep_edge = s_ref[1] != 0
    keep_partner = s_ref[2] != 0
    for side in range(2):
        @pl.when(s_ref[0] == side)
        def _fill():
            mine = slice(side * half, (side + 1) * half)
            other = slice((1 - side) * half, (2 - side) * half)
            for h, cols in enumerate((mine, other)):
                e = edge_v[:, cols]
                p = partner_v[:, cols]
                e = jnp.where(keep_edge, e, jnp.zeros_like(e))
                p = jnp.where(keep_partner, p, jnp.zeros_like(p))
                before, after = (e, p) if side == 0 else (p, e)
                tl_ref[h, :, :half] = before
                tl_ref[h, :, half : 2 * half] = cur_v[:, cols]
                tl_ref[h, :, 2 * half :] = after

    f32 = jnp.float32
    total = jnp.dot(tl_ref[0], wtm_v[...], preferred_element_type=f32) + jnp.dot(
        tl_ref[1], wto_v[...], preferred_element_type=f32
    )
    o_ref[...] = (cur_v[...].astype(f32) + total).astype(o_ref.dtype)


def edge_temporal(frame, w_mine, w_other, gain, shift, cur, partner, t_mine, t_other, scalars,
                  width):
    rows, channels = frame.shape
    half = w_mine.shape[2]
    outputs = w_mine.shape[3]
    group = outputs // GROUPS
    kernel = functools.partial(edge_temporal_kernel, width=width, group=group)
    weight_block = pl.BlockSpec((9 * half, outputs), lambda n, s: (0, 0))
    row_block = pl.BlockSpec((1, outputs), lambda n, s: (0, 0))
    anywhere = pl.BlockSpec(memory_space=pl.ANY)
    return pl.pallas_call(
        kernel,
        out_shape=jax.ShapeDtypeStruct((rows, outputs), jnp.bfloat16),
        grid_spec=pltpu.PrefetchScalarGridSpec(
            num_scalar_prefetch=1,
            grid=(1,),
            in_specs=[
                pl.BlockSpec((rows, half), lambda n, s: (0, s[0])),
                pl.BlockSpec((rows, half), lambda n, s: (0, 1 - s[0])),
                weight_block,
                weight_block,
                row_block,
                row_block,
                anywhere,
                anywhere,
                anywhere,
                anywhere,
            ],
            out_specs=pl.BlockSpec((rows, outputs), lambda n, s: (0, 0)),
            scratch_shapes=[
                pltpu.VMEM((2, rows, 9 * half), jnp.bfloat16),
                pltpu.VMEM((rows, outputs), jnp.bfloat16),
                pltpu.VMEM((rows, channels), jnp.bfloat16),
                pltpu.VMEM((rows, channels), jnp.bfloat16),
                pltpu.VMEM((3 * half, outputs), jnp.bfloat16),
                pltpu.VMEM((3 * half, outputs), jnp.bfloat16),
                pltpu.VMEM((2, rows, 3 * half), jnp.bfloat16),
                pltpu.SemaphoreType.DMA((4,)),
            ],
        ),
        compiler_params=pltpu.CompilerParams(dimension_semantics=("arbitrary",)),
    )(scalars, frame, frame, w_mine.reshape(9 * half, outputs), w_other.reshape(9 * half, outputs),
      gain, shift, cur, partner, t_mine.reshape(3 * half, outputs),
      t_other.reshape(3 * half, outputs))


def body(video, w_spatial, norm_gain, norm_shift, w_time):
    count, height, width, channels = video.shape
    assert count == 1 and lax.axis_size("fsdp") == 2
    pixels = height * width
    side = lax.axis_index("fsdp")
    blocks = lax.axis_size("video") * 2
    position = lax.axis_index("video") * 2 + side

    route = []
    for j in range(blocks):
        target = j + 1 if j % 2 == 1 else j - 1
        if 0 <= target < blocks and min(j, target) % CLIP != CLIP - 1:
            route.append((j, target))
    frame = video.reshape(pixels, channels)
    edge_video = lax.ppermute(frame, ("video", "fsdp"), route)
    other_spatial = swap_pair(w_spatial)
    other_time = swap_pair(w_time)

    gain = norm_gain.reshape(1, channels)
    shift = norm_shift.reshape(1, channels)
    sides = side.reshape(1).astype(jnp.int32)
    hidden = conv_norm(frame, w_spatial, other_spatial, gain, shift, sides, width)
    partner = swap_pair(hidden)
    keep_prev = (position % CLIP != 0).astype(jnp.int32)
    keep_next = (position % CLIP != CLIP - 1).astype(jnp.int32)
    keep_edge = jnp.where(side == 0, keep_prev, keep_next)
    keep_partner = jnp.where(side == 0, keep_next, keep_prev)
    scalars = jnp.stack([side.astype(jnp.int32), keep_edge, keep_partner])
    result = edge_temporal(edge_video, w_spatial, other_spatial, gain, shift, hidden, partner,
                           w_time, other_time, scalars, width)
    return result.reshape(count, height, width, channels)


def solution(mesh):
    placed = (
        P(("groups", "video", "fsdp"), None, None, None),
        P(None, None, "fsdp", None),
        P(),
        P(),
        P(None, "fsdp", None),
    )
    return jax.shard_map(
        body,
        mesh=mesh,
        in_specs=placed,
        out_specs=P(("groups", "video", "fsdp"), None, None, None),
        check_vma=False,
    )
```

```python
import functools

import jax
import jax.numpy as jnp
from jax import lax
from jax.experimental import pallas as pl
from jax.experimental.pallas import tpu as pltpu
from jax.sharding import PartitionSpec as P

GROUPS = 32
CLIP = 16
EPS = 1e-05


def swap_pair(block):
    return lax.ppermute(block, "fsdp", [(0, 1), (1, 0)])


def group_sum(row, size):
    lanes = lax.broadcasted_iota(jnp.int32, row.shape, 1)
    width = row.shape[1]
    step = 1
    while step < size:
        up = pltpu.roll(row, width - step, 1)
        down = pltpu.roll(row, step, 1)
        row = row + jnp.where((lanes & step) == 0, up, down)
        step *= 2
    return row


def conv_norm_kernel(side_ref, xa_ref, xb_ref, wa_ref, wb_ref, gain_ref, shift_ref, o_ref,
                     lhs_ref, *, width, group):
    rows, half = xa_ref.shape

    @pl.when(pl.program_id(0) == 0)
    def _prepare():
        col = lax.broadcasted_iota(jnp.int32, (rows, half), 0) % width
        zeros = jnp.zeros((width, half), jnp.bfloat16)
        for h, x_ref in enumerate((xa_ref, xb_ref)):
            xf = x_ref[...].astype(jnp.float32)
            left = jnp.where(col == 0, 0.0, pltpu.roll(xf, 1, 0)).astype(jnp.bfloat16)
            right = jnp.where(col == width - 1, 0.0, pltpu.roll(xf, rows - 1, 0)).astype(jnp.bfloat16)
            for dx, v in enumerate((left, xf.astype(jnp.bfloat16), right)):
                for dy in range(3):
                    lo = (dy * 3 + dx) * half
                    cols = slice(lo, lo + half)
                    if dy == 0:
                        lhs_ref[h, :width, cols] = zeros
                        lhs_ref[h, width:, cols] = v[: rows - width]
                    elif dy == 1:
                        lhs_ref[h, :, cols] = v
                    else:
                        lhs_ref[h, : rows - width, cols] = v[width:]
                        lhs_ref[h, rows - width :, cols] = zeros

    acc = jnp.dot(lhs_ref[0], wa_ref[...], preferred_element_type=jnp.float32) + jnp.dot(
        lhs_ref[1], wb_ref[...], preferred_element_type=jnp.float32
    )
    count = rows * group
    total = jnp.broadcast_to(jnp.sum(acc, axis=0, keepdims=True), (8, acc.shape[1]))
    mean = group_sum(total, group)[0:1] / count
    d = acc - mean
    spread = jnp.broadcast_to(jnp.sum(d * d, axis=0, keepdims=True), (8, acc.shape[1]))
    variance = group_sum(spread, group)[0:1] / count
    v = d * lax.rsqrt(variance + EPS) * gain_ref[...] + shift_ref[...]
    o_ref[...] = (v / (1.0 + jnp.exp(-v))).astype(o_ref.dtype)


def conv_norm(frame, w_mine, w_other, gain, shift, side, width, split=1):
    rows, channels = frame.shape
    half = w_mine.shape[2]
    outputs = w_mine.shape[3]
    group = outputs // GROUPS
    block = outputs // split
    kernel = functools.partial(conv_norm_kernel, width=width, group=group)
    weight_block = pl.BlockSpec(memory_space=pltpu.VMEM)
    row_block = pl.BlockSpec((1, block), lambda n, s: (0, n))
    return pl.pallas_call(
        kernel,
        out_shape=jax.ShapeDtypeStruct((rows, outputs), jnp.bfloat16),
        grid_spec=pltpu.PrefetchScalarGridSpec(
            num_scalar_prefetch=1,
            grid=(split,),
            in_specs=[
                pl.BlockSpec((rows, half), lambda n, s: (0, s[0])),
                pl.BlockSpec((rows, half), lambda n, s: (0, 1 - s[0])),
                weight_block,
                weight_block,
                row_block,
                row_block,
            ],
            out_specs=pl.BlockSpec((rows, block), lambda n, s: (0, n)),
            scratch_shapes=[pltpu.VMEM((2, rows, 9 * half), jnp.bfloat16)],
        ),
        compiler_params=pltpu.CompilerParams(dimension_semantics=("arbitrary",)),
    )(side, frame, frame, w_mine.reshape(9 * half, outputs), w_other.reshape(9 * half, outputs),
      gain, shift)


def edge_temporal_kernel(s_ref, xa_ref, xb_ref, wa_ref, wb_ref, gain_ref, shift_ref,
                         cur_hbm, partner_hbm, wtm_hbm, wto_hbm, o_ref,
                         lhs_ref, edge_v, cur_v, partner_v, wtm_v, wto_v, tl_ref, sem,
                         *, width, group):
    copies = [
        pltpu.make_async_copy(src, dst, sem.at[i])
        for i, (src, dst) in enumerate(
            ((cur_hbm, cur_v), (partner_hbm, partner_v), (wtm_hbm, wtm_v), (wto_hbm, wto_v))
        )
    ]
    for copy in copies:
        copy.start()
    conv_norm_kernel(s_ref, xa_ref, xb_ref, wa_ref, wb_ref, gain_ref, shift_ref, edge_v,
                     lhs_ref, width=width, group=group)
    for copy in copies:
        copy.wait()

    rows, half = xa_ref.shape
    keep_edge = s_ref[1] != 0
    keep_partner = s_ref[2] != 0
    for side in range(2):
        @pl.when(s_ref[0] == side)
        def _fill():
            mine = slice(side * half, (side + 1) * half)
            other = slice((1 - side) * half, (2 - side) * half)
            for h, cols in enumerate((mine, other)):
                e = edge_v[:, cols]
                p = partner_v[:, cols]
                e = jnp.where(keep_edge, e, jnp.zeros_like(e))
                p = jnp.where(keep_partner, p, jnp.zeros_like(p))
                before, after = (e, p) if side == 0 else (p, e)
                tl_ref[h, :, :half] = before
                tl_ref[h, :, half : 2 * half] = cur_v[:, cols]
                tl_ref[h, :, 2 * half :] = after

    f32 = jnp.float32
    total = jnp.dot(tl_ref[0], wtm_v[...], preferred_element_type=f32) + jnp.dot(
        tl_ref[1], wto_v[...], preferred_element_type=f32
    )
    o_ref[...] = (cur_v[...].astype(f32) + total).astype(o_ref.dtype)


def edge_temporal(frame, w_mine, w_other, gain, shift, cur, partner, t_mine, t_other, scalars,
                  width):
    rows, channels = frame.shape
    half = w_mine.shape[2]
    outputs = w_mine.shape[3]
    group = outputs // GROUPS
    kernel = functools.partial(edge_temporal_kernel, width=width, group=group)
    weight_block = pl.BlockSpec(memory_space=pltpu.VMEM)
    row_block = pl.BlockSpec((1, outputs), lambda n, s: (0, 0))
    anywhere = pl.BlockSpec(memory_space=pl.ANY)
    return pl.pallas_call(
        kernel,
        out_shape=jax.ShapeDtypeStruct((rows, outputs), jnp.bfloat16),
        grid_spec=pltpu.PrefetchScalarGridSpec(
            num_scalar_prefetch=1,
            grid=(1,),
            in_specs=[
                pl.BlockSpec((rows, half), lambda n, s: (0, s[0])),
                pl.BlockSpec((rows, half), lambda n, s: (0, 1 - s[0])),
                weight_block,
                weight_block,
                row_block,
                row_block,
                anywhere,
                anywhere,
                anywhere,
                anywhere,
            ],
            out_specs=pl.BlockSpec((rows, outputs), lambda n, s: (0, 0)),
            scratch_shapes=[
                pltpu.VMEM((2, rows, 9 * half), jnp.bfloat16),
                pltpu.VMEM((rows, outputs), jnp.bfloat16),
                pltpu.VMEM((rows, channels), jnp.bfloat16),
                pltpu.VMEM((rows, channels), jnp.bfloat16),
                pltpu.VMEM((3 * half, outputs), jnp.bfloat16),
                pltpu.VMEM((3 * half, outputs), jnp.bfloat16),
                pltpu.VMEM((2, rows, 3 * half), jnp.bfloat16),
                pltpu.SemaphoreType.DMA((4,)),
            ],
        ),
        compiler_params=pltpu.CompilerParams(dimension_semantics=("arbitrary",)),
    )(scalars, frame, frame, w_mine.reshape(9 * half, outputs), w_other.reshape(9 * half, outputs),
      gain, shift, cur, partner, t_mine.reshape(3 * half, outputs),
      t_other.reshape(3 * half, outputs))


def body(video, w_spatial, norm_gain, norm_shift, w_time):
    count, height, width, channels = video.shape
    assert count == 1 and lax.axis_size("fsdp") == 2
    pixels = height * width
    side = lax.axis_index("fsdp")
    blocks = lax.axis_size("video") * 2
    position = lax.axis_index("video") * 2 + side

    route = []
    for j in range(blocks):
        target = j + 1 if j % 2 == 1 else j - 1
        if 0 <= target < blocks and min(j, target) % CLIP != CLIP - 1:
            route.append((j, target))
    frame = video.reshape(pixels, channels)
    edge_video = lax.ppermute(frame, ("video", "fsdp"), route)
    other_spatial = swap_pair(w_spatial)
    other_time = swap_pair(w_time)

    gain = norm_gain.reshape(1, channels)
    shift = norm_shift.reshape(1, channels)
    sides = side.reshape(1).astype(jnp.int32)
    hidden = conv_norm(frame, w_spatial, other_spatial, gain, shift, sides, width)
    partner = swap_pair(hidden)
    keep_prev = (position % CLIP != 0).astype(jnp.int32)
    keep_next = (position % CLIP != CLIP - 1).astype(jnp.int32)
    keep_edge = jnp.where(side == 0, keep_prev, keep_next)
    keep_partner = jnp.where(side == 0, keep_next, keep_prev)
    scalars = jnp.stack([side.astype(jnp.int32), keep_edge, keep_partner])
    result = edge_temporal(edge_video, w_spatial, other_spatial, gain, shift, hidden, partner,
                           w_time, other_time, scalars, width)
    return result.reshape(count, height, width, channels)


def solution(mesh):
    placed = (
        P(("groups", "video", "fsdp"), None, None, None),
        P(None, None, "fsdp", None),
        P(),
        P(),
        P(None, "fsdp", None),
    )
    return jax.shard_map(
        body,
        mesh=mesh,
        in_specs=placed,
        out_specs=P(("groups", "video", "fsdp"), None, None, None),
        check_vma=False,
    )
```

```python
import functools

import jax
import jax.numpy as jnp
from jax import lax
from jax.experimental import pallas as pl
from jax.experimental.pallas import tpu as pltpu
from jax.sharding import PartitionSpec as P

GROUPS = 32
CLIP = 16
EPS = 1e-05


def swap_pair(block):
    return lax.ppermute(block, "fsdp", [(0, 1), (1, 0)])


def group_sum(row, size):
    lanes = lax.broadcasted_iota(jnp.int32, row.shape, 1)
    width = row.shape[1]
    step = 1
    while step < size:
        up = pltpu.roll(row, width - step, 1)
        down = pltpu.roll(row, step, 1)
        row = row + jnp.where((lanes & step) == 0, up, down)
        step *= 2
    return row


def build_lhs(halves, lhs_ref, width):
    rows, half = halves[0][1].shape
    col = lax.broadcasted_iota(jnp.int32, (rows, half), 0) % width
    zeros = jnp.zeros((width, half), jnp.bfloat16)
    for h, x in halves:
        xf = x.astype(jnp.float32)
        left = jnp.where(col == 0, 0.0, pltpu.roll(xf, 1, 0)).astype(jnp.bfloat16)
        right = jnp.where(col == width - 1, 0.0, pltpu.roll(xf, rows - 1, 0)).astype(jnp.bfloat16)
        for dx, v in enumerate((left, xf.astype(jnp.bfloat16), right)):
            for dy in range(3):
                lo = (dy * 3 + dx) * half
                cols = slice(lo, lo + half)
                if dy == 0:
                    lhs_ref[h, :width, cols] = zeros
                    lhs_ref[h, width:, cols] = v[: rows - width]
                elif dy == 1:
                    lhs_ref[h, :, cols] = v
                else:
                    lhs_ref[h, : rows - width, cols] = v[width:]
                    lhs_ref[h, rows - width :, cols] = zeros


def own_conv_kernel(side_ref, xa_ref, xb_ref, wa_ref, wb_ref, gain_ref, shift_ref, later_hbm,
                    o_ref, lhs_ref, *, width, group):
    conv_norm_kernel(side_ref, xa_ref, xb_ref, wa_ref, wb_ref, gain_ref, shift_ref, o_ref,
                     lhs_ref, width=width, group=group)


def conv_norm_kernel(side_ref, xa_ref, xb_ref, wa_ref, wb_ref, gain_ref, shift_ref, o_ref,
                     lhs_ref, *, width, group):
    build_lhs(((0, xa_ref[...]), (1, xb_ref[...])), lhs_ref, width)
    dots_norm(lhs_ref, wa_ref, wb_ref, gain_ref, shift_ref, o_ref, group)


def dots_norm(lhs_ref, wa_ref, wb_ref, gain_ref, shift_ref, o_ref, group):
    rows = lhs_ref.shape[1]
    acc = jnp.dot(lhs_ref[0], wa_ref[...], preferred_element_type=jnp.float32) + jnp.dot(
        lhs_ref[1], wb_ref[...], preferred_element_type=jnp.float32
    )
    count = rows * group
    total = jnp.broadcast_to(jnp.sum(acc, axis=0, keepdims=True), (8, acc.shape[1]))
    mean = group_sum(total, group)[0:1] / count
    d = acc - mean
    spread = jnp.broadcast_to(jnp.sum(d * d, axis=0, keepdims=True), (8, acc.shape[1]))
    variance = group_sum(spread, group)[0:1] / count
    v = d * lax.rsqrt(variance + EPS) * gain_ref[...] + shift_ref[...]
    o_ref[...] = (v / (1.0 + jnp.exp(-v))).astype(o_ref.dtype)


def conv_norm(frame, w_mine, w_other, gain, shift, side, width, later, split=1):
    rows, channels = frame.shape
    half = w_mine.shape[2]
    outputs = w_mine.shape[3]
    group = outputs // GROUPS
    block = outputs // split
    kernel = functools.partial(own_conv_kernel, width=width, group=group)
    weight_block = pl.BlockSpec((9 * half, block), lambda n, s: (0, n))
    row_block = pl.BlockSpec((1, block), lambda n, s: (0, n))
    return pl.pallas_call(
        kernel,
        out_shape=jax.ShapeDtypeStruct((rows, outputs), jnp.bfloat16),
        grid_spec=pltpu.PrefetchScalarGridSpec(
            num_scalar_prefetch=1,
            grid=(split,),
            in_specs=[
                pl.BlockSpec((rows, half), lambda n, s: (0, s[0])),
                pl.BlockSpec((rows, half), lambda n, s: (0, 1 - s[0])),
                weight_block,
                weight_block,
                row_block,
                row_block,
                pl.BlockSpec(memory_space=pl.ANY),
            ],
            out_specs=pl.BlockSpec((rows, block), lambda n, s: (0, n)),
            scratch_shapes=[pltpu.VMEM((2, rows, 9 * half), jnp.bfloat16)],
        ),
        compiler_params=pltpu.CompilerParams(dimension_semantics=("arbitrary",)),
    )(side, frame, frame, w_mine.reshape(9 * half, outputs), w_other.reshape(9 * half, outputs),
      gain, shift, later)


def edge_temporal_kernel(s_ref, x_ref, wa_ref, wb_ref, gain_ref, shift_ref,
                         cur_hbm, partner_hbm, wtm_hbm, wto_hbm, o_ref,
                         lhs_ref, edge_v, cur_v, partner_v, wtm_v, wto_v, tl_ref, sem,
                         *, width, group):
    copies = [
        pltpu.make_async_copy(src, dst, sem.at[i])
        for i, (src, dst) in enumerate(
            ((cur_hbm, cur_v), (partner_hbm, partner_v), (wtm_hbm, wtm_v), (wto_hbm, wto_v))
        )
    ]
    for copy in copies:
        copy.start()
    half = x_ref.shape[1] // 2
    build_lhs(
        [((h + s_ref[0]) % 2, x_ref[:, h * half : (h + 1) * half]) for h in range(2)], lhs_ref, width
    )
    dots_norm(lhs_ref, wa_ref, wb_ref, gain_ref, shift_ref, edge_v, group)
    for copy in copies:
        copy.wait()

    rows = x_ref.shape[0]
    keep_edge = s_ref[1] != 0
    keep_partner = s_ref[2] != 0
    for side in range(2):
        @pl.when(s_ref[0] == side)
        def _fill():
            mine = slice(side * half, (side + 1) * half)
            other = slice((1 - side) * half, (2 - side) * half)
            for h, cols in enumerate((mine, other)):
                e = edge_v[:, cols]
                p = partner_v[:, cols]
                e = jnp.where(keep_edge, e, jnp.zeros_like(e))
                p = jnp.where(keep_partner, p, jnp.zeros_like(p))
                before, after = (e, p) if side == 0 else (p, e)
                tl_ref[h, :, :half] = before
                tl_ref[h, :, half : 2 * half] = cur_v[:, cols]
                tl_ref[h, :, 2 * half :] = after

    f32 = jnp.float32
    total = jnp.dot(tl_ref[0], wtm_v[...], preferred_element_type=f32) + jnp.dot(
        tl_ref[1], wto_v[...], preferred_element_type=f32
    )
    o_ref[...] = (cur_v[...].astype(f32) + total).astype(o_ref.dtype)


def edge_temporal(frame, w_mine, w_other, gain, shift, cur, partner, t_mine, t_other, scalars,
                  width):
    rows, channels = frame.shape
    half = w_mine.shape[2]
    outputs = w_mine.shape[3]
    group = outputs // GROUPS
    kernel = functools.partial(edge_temporal_kernel, width=width, group=group)
    weight_block = pl.BlockSpec((9 * half, outputs), lambda n, s: (0, 0))
    row_block = pl.BlockSpec((1, outputs), lambda n, s: (0, 0))
    anywhere = pl.BlockSpec(memory_space=pl.ANY)
    in_vmem = pl.BlockSpec(memory_space=pltpu.VMEM)
    return pl.pallas_call(
        kernel,
        out_shape=jax.ShapeDtypeStruct((rows, outputs), jnp.bfloat16),
        grid_spec=pltpu.PrefetchScalarGridSpec(
            num_scalar_prefetch=1,
            grid=(1,),
            in_specs=[
                in_vmem,
                weight_block,
                weight_block,
                row_block,
                row_block,
                anywhere,
                anywhere,
                anywhere,
                anywhere,
            ],
            out_specs=pl.BlockSpec((rows, outputs), lambda n, s: (0, 0)),
            scratch_shapes=[
                pltpu.VMEM((2, rows, 9 * half), jnp.bfloat16),
                pltpu.VMEM((rows, outputs), jnp.bfloat16),
                pltpu.VMEM((rows, channels), jnp.bfloat16),
                pltpu.VMEM((rows, channels), jnp.bfloat16),
                pltpu.VMEM((3 * half, outputs), jnp.bfloat16),
                pltpu.VMEM((3 * half, outputs), jnp.bfloat16),
                pltpu.VMEM((2, rows, 3 * half), jnp.bfloat16),
                pltpu.SemaphoreType.DMA((4,)),
            ],
        ),
        compiler_params=pltpu.CompilerParams(dimension_semantics=("arbitrary",)),
    )(scalars, frame, w_mine.reshape(9 * half, outputs), w_other.reshape(9 * half, outputs),
      gain, shift, cur, partner, t_mine.reshape(3 * half, outputs),
      t_other.reshape(3 * half, outputs))


def body(video, w_spatial, norm_gain, norm_shift, w_time):
    count, height, width, channels = video.shape
    assert count == 1 and lax.axis_size("fsdp") == 2
    pixels = height * width
    side = lax.axis_index("fsdp")
    blocks = lax.axis_size("video") * 2
    position = lax.axis_index("video") * 2 + side

    route = []
    for j in range(blocks):
        target = j + 1 if j % 2 == 1 else j - 1
        if 0 <= target < blocks and min(j, target) % CLIP != CLIP - 1:
            route.append((j, target))
    frame = video.reshape(pixels, channels)
    edge_video = lax.ppermute(frame, ("video", "fsdp"), route)
    other_spatial = swap_pair(w_spatial)
    other_time = swap_pair(w_time)

    gain = norm_gain.reshape(1, channels)
    shift = norm_shift.reshape(1, channels)
    sides = side.reshape(1).astype(jnp.int32)
    hidden = conv_norm(frame, w_spatial, other_spatial, gain, shift, sides, width, other_time)
    partner = swap_pair(hidden)
    keep_prev = (position % CLIP != 0).astype(jnp.int32)
    keep_next = (position % CLIP != CLIP - 1).astype(jnp.int32)
    keep_edge = jnp.where(side == 0, keep_prev, keep_next)
    keep_partner = jnp.where(side == 0, keep_next, keep_prev)
    scalars = jnp.stack([side.astype(jnp.int32), keep_edge, keep_partner])
    result = edge_temporal(edge_video, w_spatial, other_spatial, gain, shift, hidden, partner,
                           w_time, other_time, scalars, width)
    return result.reshape(count, height, width, channels)


def solution(mesh):
    placed = (
        P(("groups", "video", "fsdp"), None, None, None),
        P(None, None, "fsdp", None),
        P(),
        P(),
        P(None, "fsdp", None),
    )
    return jax.shard_map(
        body,
        mesh=mesh,
        in_specs=placed,
        out_specs=P(("groups", "video", "fsdp"), None, None, None),
        check_vma=False,
    )
```

```python
import functools

import jax
import jax.numpy as jnp
from jax import lax
from jax.experimental import pallas as pl
from jax.experimental.pallas import tpu as pltpu
from jax.sharding import PartitionSpec as P

GROUPS = 32
CLIP = 16
EPS = 1e-05


def swap_pair(block):
    return lax.ppermute(block, "fsdp", [(0, 1), (1, 0)])


def group_sum(row, size):
    lanes = lax.broadcasted_iota(jnp.int32, row.shape, 1)
    width = row.shape[1]
    step = 1
    while step < size:
        up = pltpu.roll(row, width - step, 1)
        down = pltpu.roll(row, step, 1)
        row = row + jnp.where((lanes & step) == 0, up, down)
        step *= 2
    return row


def build_lhs(halves, lhs_ref, width):
    rows, half = halves[0][1].shape
    col = lax.broadcasted_iota(jnp.int32, (rows, half), 0) % width
    zeros = jnp.zeros((width, half), jnp.bfloat16)
    for h, x in halves:
        xf = x.astype(jnp.float32)
        left = jnp.where(col == 0, 0.0, pltpu.roll(xf, 1, 0)).astype(jnp.bfloat16)
        right = jnp.where(col == width - 1, 0.0, pltpu.roll(xf, rows - 1, 0)).astype(jnp.bfloat16)
        for dx, v in enumerate((left, xf.astype(jnp.bfloat16), right)):
            for dy in range(3):
                lo = (dy * 3 + dx) * half
                cols = slice(lo, lo + half)
                if dy == 0:
                    lhs_ref[h, :width, cols] = zeros
                    lhs_ref[h, width:, cols] = v[: rows - width]
                elif dy == 1:
                    lhs_ref[h, :, cols] = v
                else:
                    lhs_ref[h, : rows - width, cols] = v[width:]
                    lhs_ref[h, rows - width :, cols] = zeros


def own_conv_kernel(side_ref, xa_ref, xb_ref, wa_ref, wb_ref, gain_ref, shift_ref, later_hbm,
                    o_ref, lhs_ref, *, width, group):
    conv_norm_kernel(side_ref, xa_ref, xb_ref, wa_ref, wb_ref, gain_ref, shift_ref, o_ref,
                     lhs_ref, width=width, group=group)


def conv_norm_kernel(side_ref, xa_ref, xb_ref, wa_ref, wb_ref, gain_ref, shift_ref, o_ref,
                     lhs_ref, *, width, group):
    build_lhs(((0, xa_ref[...]), (1, xb_ref[...])), lhs_ref, width)
    dots_norm(lhs_ref, wa_ref, wb_ref, gain_ref, shift_ref, o_ref, group)


def dots_norm(lhs_ref, wa_ref, wb_ref, gain_ref, shift_ref, o_ref, group):
    rows = lhs_ref.shape[1]
    acc = jnp.dot(lhs_ref[0], wa_ref[...], preferred_element_type=jnp.float32) + jnp.dot(
        lhs_ref[1], wb_ref[...], preferred_element_type=jnp.float32
    )
    count = rows * group
    total = jnp.broadcast_to(jnp.sum(acc, axis=0, keepdims=True), (8, acc.shape[1]))
    mean = group_sum(total, group)[0:1] / count
    d = acc - mean
    spread = jnp.broadcast_to(jnp.sum(d * d, axis=0, keepdims=True), (8, acc.shape[1]))
    variance = group_sum(spread, group)[0:1] / count
    v = d * lax.rsqrt(variance + EPS) * gain_ref[...] + shift_ref[...]
    o_ref[...] = (v / (1.0 + jnp.exp(-v))).astype(o_ref.dtype)


def conv_norm(frame, w_mine, w_other, gain, shift, side, width, later, split=1):
    rows, channels = frame.shape
    half = w_mine.shape[2]
    outputs = w_mine.shape[3]
    group = outputs // GROUPS
    block = outputs // split
    kernel = functools.partial(own_conv_kernel, width=width, group=group)
    weight_block = pl.BlockSpec((9 * half, block), lambda n, s: (0, n))
    row_block = pl.BlockSpec((1, block), lambda n, s: (0, n))
    return pl.pallas_call(
        kernel,
        out_shape=jax.ShapeDtypeStruct((rows, outputs), jnp.bfloat16),
        grid_spec=pltpu.PrefetchScalarGridSpec(
            num_scalar_prefetch=1,
            grid=(split,),
            in_specs=[
                pl.BlockSpec((rows, half), lambda n, s: (0, s[0])),
                pl.BlockSpec((rows, half), lambda n, s: (0, 1 - s[0])),
                weight_block,
                weight_block,
                row_block,
                row_block,
                pl.BlockSpec(memory_space=pl.ANY),
            ],
            out_specs=pl.BlockSpec((rows, block), lambda n, s: (0, n)),
            scratch_shapes=[pltpu.VMEM((2, rows, 9 * half), jnp.bfloat16)],
        ),
        compiler_params=pltpu.CompilerParams(dimension_semantics=("arbitrary",)),
    )(side, frame, frame, w_mine.reshape(9 * half, outputs), w_other.reshape(9 * half, outputs),
      gain, shift, later)


def edge_temporal_kernel(s_ref, x_ref, wa_ref, wb_ref, gain_ref, shift_ref,
                         cur_hbm, partner_v, wtm_hbm, wto_hbm, o_ref,
                         lhs_ref, edge_v, cur_v, wtm_v, wto_v, tl_ref, sem,
                         *, width, group):
    copies = [
        pltpu.make_async_copy(src, dst, sem.at[i])
        for i, (src, dst) in enumerate(
            ((cur_hbm, cur_v), (wtm_hbm, wtm_v), (wto_hbm, wto_v))
        )
    ]
    for copy in copies:
        copy.start()
    half = x_ref.shape[1] // 2
    build_lhs(
        [((h + s_ref[0]) % 2, x_ref[:, h * half : (h + 1) * half]) for h in range(2)], lhs_ref, width
    )
    dots_norm(lhs_ref, wa_ref, wb_ref, gain_ref, shift_ref, edge_v, group)
    for copy in copies:
        copy.wait()

    rows = x_ref.shape[0]
    keep_edge = s_ref[1] != 0
    keep_partner = s_ref[2] != 0
    for side in range(2):
        @pl.when(s_ref[0] == side)
        def _fill():
            mine = slice(side * half, (side + 1) * half)
            other = slice((1 - side) * half, (2 - side) * half)
            for h, cols in enumerate((mine, other)):
                e = edge_v[:, cols]
                p = partner_v[:, cols]
                e = jnp.where(keep_edge, e, jnp.zeros_like(e))
                p = jnp.where(keep_partner, p, jnp.zeros_like(p))
                before, after = (e, p) if side == 0 else (p, e)
                tl_ref[h, :, :half] = before
                tl_ref[h, :, half : 2 * half] = cur_v[:, cols]
                tl_ref[h, :, 2 * half :] = after

    f32 = jnp.float32
    total = jnp.dot(tl_ref[0], wtm_v[...], preferred_element_type=f32) + jnp.dot(
        tl_ref[1], wto_v[...], preferred_element_type=f32
    )
    o_ref[...] = (cur_v[...].astype(f32) + total).astype(o_ref.dtype)


def edge_temporal(frame, w_mine, w_other, gain, shift, cur, partner, t_mine, t_other, scalars,
                  width):
    rows, channels = frame.shape
    half = w_mine.shape[2]
    outputs = w_mine.shape[3]
    group = outputs // GROUPS
    kernel = functools.partial(edge_temporal_kernel, width=width, group=group)
    weight_block = pl.BlockSpec((9 * half, outputs), lambda n, s: (0, 0))
    row_block = pl.BlockSpec((1, outputs), lambda n, s: (0, 0))
    anywhere = pl.BlockSpec(memory_space=pl.ANY)
    in_vmem = pl.BlockSpec(memory_space=pltpu.VMEM)
    return pl.pallas_call(
        kernel,
        out_shape=jax.ShapeDtypeStruct((rows, outputs), jnp.bfloat16),
        grid_spec=pltpu.PrefetchScalarGridSpec(
            num_scalar_prefetch=1,
            grid=(1,),
            in_specs=[
                in_vmem,
                weight_block,
                weight_block,
                row_block,
                row_block,
                anywhere,
                in_vmem,
                anywhere,
                anywhere,
            ],
            out_specs=pl.BlockSpec((rows, outputs), lambda n, s: (0, 0)),
            scratch_shapes=[
                pltpu.VMEM((2, rows, 9 * half), jnp.bfloat16),
                pltpu.VMEM((rows, outputs), jnp.bfloat16),
                pltpu.VMEM((rows, channels), jnp.bfloat16),
                pltpu.VMEM((3 * half, outputs), jnp.bfloat16),
                pltpu.VMEM((3 * half, outputs), jnp.bfloat16),
                pltpu.VMEM((2, rows, 3 * half), jnp.bfloat16),
                pltpu.SemaphoreType.DMA((3,)),
            ],
        ),
        compiler_params=pltpu.CompilerParams(dimension_semantics=("arbitrary",)),
    )(scalars, frame, w_mine.reshape(9 * half, outputs), w_other.reshape(9 * half, outputs),
      gain, shift, cur, partner, t_mine.reshape(3 * half, outputs),
      t_other.reshape(3 * half, outputs))


def body(video, w_spatial, norm_gain, norm_shift, w_time):
    count, height, width, channels = video.shape
    assert count == 1 and lax.axis_size("fsdp") == 2
    pixels = height * width
    side = lax.axis_index("fsdp")
    blocks = lax.axis_size("video") * 2
    position = lax.axis_index("video") * 2 + side

    route = []
    for j in range(blocks):
        target = j + 1 if j % 2 == 1 else j - 1
        if 0 <= target < blocks and min(j, target) % CLIP != CLIP - 1:
            route.append((j, target))
    frame = video.reshape(pixels, channels)
    edge_video = lax.ppermute(frame, ("video", "fsdp"), route)
    other_spatial = swap_pair(w_spatial)
    other_time = swap_pair(w_time)

    gain = norm_gain.reshape(1, channels)
    shift = norm_shift.reshape(1, channels)
    sides = side.reshape(1).astype(jnp.int32)
    hidden = conv_norm(frame, w_spatial, other_spatial, gain, shift, sides, width, other_time)
    partner = swap_pair(hidden)
    keep_prev = (position % CLIP != 0).astype(jnp.int32)
    keep_next = (position % CLIP != CLIP - 1).astype(jnp.int32)
    keep_edge = jnp.where(side == 0, keep_prev, keep_next)
    keep_partner = jnp.where(side == 0, keep_next, keep_prev)
    scalars = jnp.stack([side.astype(jnp.int32), keep_edge, keep_partner])
    result = edge_temporal(edge_video, w_spatial, other_spatial, gain, shift, hidden, partner,
                           w_time, other_time, scalars, width)
    return result.reshape(count, height, width, channels)


def solution(mesh):
    placed = (
        P(("groups", "video", "fsdp"), None, None, None),
        P(None, None, "fsdp", None),
        P(),
        P(),
        P(None, "fsdp", None),
    )
    return jax.shard_map(
        body,
        mesh=mesh,
        in_specs=placed,
        out_specs=P(("groups", "video", "fsdp"), None, None, None),
        check_vma=False,
    )
```

```python
import functools

import jax
import jax.numpy as jnp
from jax import lax
from jax.experimental import pallas as pl
from jax.experimental.pallas import tpu as pltpu
from jax.sharding import PartitionSpec as P

GROUPS = 32
CLIP = 16
EPS = 1e-05


def swap_pair(block):
    return lax.ppermute(block, "fsdp", [(0, 1), (1, 0)])


def group_sum(row, size):
    lanes = lax.broadcasted_iota(jnp.int32, row.shape, 1)
    width = row.shape[1]
    step = 1
    while step < size:
        up = pltpu.roll(row, width - step, 1)
        down = pltpu.roll(row, step, 1)
        row = row + jnp.where((lanes & step) == 0, up, down)
        step *= 2
    return row


def conv_norm_kernel(side_ref, xa_ref, xb_ref, wa_ref, wb_ref, gain_ref, shift_ref, o_ref,
                     lhs_ref, *, width, group):
    rows, half = xa_ref.shape

    @pl.when(pl.program_id(0) == 0)
    def _prepare():
        col = lax.broadcasted_iota(jnp.int32, (rows, half), 0) % width
        zeros = jnp.zeros((width, half), jnp.bfloat16)
        for h, x_ref in enumerate((xa_ref, xb_ref)):
            xf = x_ref[...].astype(jnp.float32)
            left = jnp.where(col == 0, 0.0, pltpu.roll(xf, 1, 0)).astype(jnp.bfloat16)
            right = jnp.where(col == width - 1, 0.0, pltpu.roll(xf, rows - 1, 0)).astype(jnp.bfloat16)
            for dx, v in enumerate((left, xf.astype(jnp.bfloat16), right)):
                for dy in range(3):
                    lo = (dy * 3 + dx) * half
                    cols = slice(lo, lo + half)
                    if dy == 0:
                        lhs_ref[h, :width, cols] = zeros
                        lhs_ref[h, width:, cols] = v[: rows - width]
                    elif dy == 1:
                        lhs_ref[h, :, cols] = v
                    else:
                        lhs_ref[h, : rows - width, cols] = v[width:]
                        lhs_ref[h, rows - width :, cols] = zeros

    acc = jnp.dot(lhs_ref[0], wa_ref[...], preferred_element_type=jnp.float32) + jnp.dot(
        lhs_ref[1], wb_ref[...], preferred_element_type=jnp.float32
    )
    count = rows * group
    total = jnp.broadcast_to(jnp.sum(acc, axis=0, keepdims=True), (8, acc.shape[1]))
    mean = group_sum(total, group)[0:1] / count
    d = acc - mean
    spread = jnp.broadcast_to(jnp.sum(d * d, axis=0, keepdims=True), (8, acc.shape[1]))
    variance = group_sum(spread, group)[0:1] / count
    v = d * lax.rsqrt(variance + EPS) * gain_ref[...] + shift_ref[...]
    half_v = 0.5 * v
    o_ref[...] = (half_v + half_v * jnp.tanh(half_v)).astype(o_ref.dtype)


def conv_norm(frame, w_mine, w_other, gain, shift, side, width, split=1):
    rows, channels = frame.shape
    half = w_mine.shape[2]
    outputs = w_mine.shape[3]
    group = outputs // GROUPS
    block = outputs // split
    kernel = functools.partial(conv_norm_kernel, width=width, group=group)
    weight_block = pl.BlockSpec((9 * half, block), lambda n, s: (0, n))
    row_block = pl.BlockSpec((1, block), lambda n, s: (0, n))
    return pl.pallas_call(
        kernel,
        out_shape=jax.ShapeDtypeStruct((rows, outputs), jnp.bfloat16),
        grid_spec=pltpu.PrefetchScalarGridSpec(
            num_scalar_prefetch=1,
            grid=(split,),
            in_specs=[
                pl.BlockSpec((rows, half), lambda n, s: (0, s[0])),
                pl.BlockSpec((rows, half), lambda n, s: (0, 1 - s[0])),
                weight_block,
                weight_block,
                row_block,
                row_block,
            ],
            out_specs=pl.BlockSpec((rows, block), lambda n, s: (0, n)),
            scratch_shapes=[pltpu.VMEM((2, rows, 9 * half), jnp.bfloat16)],
        ),
        compiler_params=pltpu.CompilerParams(dimension_semantics=("arbitrary",)),
    )(side, frame, frame, w_mine.reshape(9 * half, outputs), w_other.reshape(9 * half, outputs),
      gain, shift)


def edge_temporal_kernel(s_ref, xa_ref, xb_ref, wa_ref, wb_ref, gain_ref, shift_ref,
                         cur_hbm, partner_hbm, wtm_hbm, wto_hbm, o_ref,
                         lhs_ref, edge_v, cur_v, partner_v, wtm_v, wto_v, tl_ref, sem,
                         *, width, group):
    copies = [
        pltpu.make_async_copy(src, dst, sem.at[i])
        for i, (src, dst) in enumerate(
            ((cur_hbm, cur_v), (partner_hbm, partner_v), (wtm_hbm, wtm_v), (wto_hbm, wto_v))
        )
    ]
    for copy in copies:
        copy.start()
    conv_norm_kernel(s_ref, xa_ref, xb_ref, wa_ref, wb_ref, gain_ref, shift_ref, edge_v,
                     lhs_ref, width=width, group=group)
    for copy in copies:
        copy.wait()

    rows, half = xa_ref.shape
    keep_edge = s_ref[1] != 0
    keep_partner = s_ref[2] != 0
    for side in range(2):
        @pl.when(s_ref[0] == side)
        def _fill():
            mine = slice(side * half, (side + 1) * half)
            other = slice((1 - side) * half, (2 - side) * half)
            for h, cols in enumerate((mine, other)):
                e = edge_v[:, cols]
                p = partner_v[:, cols]
                e = jnp.where(keep_edge, e, jnp.zeros_like(e))
                p = jnp.where(keep_partner, p, jnp.zeros_like(p))
                before, after = (e, p) if side == 0 else (p, e)
                tl_ref[h, :, :half] = before
                tl_ref[h, :, half : 2 * half] = cur_v[:, cols]
                tl_ref[h, :, 2 * half :] = after

    f32 = jnp.float32
    total = jnp.dot(tl_ref[0], wtm_v[...], preferred_element_type=f32) + jnp.dot(
        tl_ref[1], wto_v[...], preferred_element_type=f32
    )
    o_ref[...] = (cur_v[...].astype(f32) + total).astype(o_ref.dtype)


def edge_temporal(frame, w_mine, w_other, gain, shift, cur, partner, t_mine, t_other, scalars,
                  width):
    rows, channels = frame.shape
    half = w_mine.shape[2]
    outputs = w_mine.shape[3]
    group = outputs // GROUPS
    kernel = functools.partial(edge_temporal_kernel, width=width, group=group)
    weight_block = pl.BlockSpec((9 * half, outputs), lambda n, s: (0, 0))
    row_block = pl.BlockSpec((1, outputs), lambda n, s: (0, 0))
    anywhere = pl.BlockSpec(memory_space=pl.ANY)
    return pl.pallas_call(
        kernel,
        out_shape=jax.ShapeDtypeStruct((rows, outputs), jnp.bfloat16),
        grid_spec=pltpu.PrefetchScalarGridSpec(
            num_scalar_prefetch=1,
            grid=(1,),
            in_specs=[
                pl.BlockSpec((rows, half), lambda n, s: (0, s[0])),
                pl.BlockSpec((rows, half), lambda n, s: (0, 1 - s[0])),
                weight_block,
                weight_block,
                row_block,
                row_block,
                anywhere,
                anywhere,
                anywhere,
                anywhere,
            ],
            out_specs=pl.BlockSpec((rows, outputs), lambda n, s: (0, 0)),
            scratch_shapes=[
                pltpu.VMEM((2, rows, 9 * half), jnp.bfloat16),
                pltpu.VMEM((rows, outputs), jnp.bfloat16),
                pltpu.VMEM((rows, channels), jnp.bfloat16),
                pltpu.VMEM((rows, channels), jnp.bfloat16),
                pltpu.VMEM((3 * half, outputs), jnp.bfloat16),
                pltpu.VMEM((3 * half, outputs), jnp.bfloat16),
                pltpu.VMEM((2, rows, 3 * half), jnp.bfloat16),
                pltpu.SemaphoreType.DMA((4,)),
            ],
        ),
        compiler_params=pltpu.CompilerParams(dimension_semantics=("arbitrary",)),
    )(scalars, frame, frame, w_mine.reshape(9 * half, outputs), w_other.reshape(9 * half, outputs),
      gain, shift, cur, partner, t_mine.reshape(3 * half, outputs),
      t_other.reshape(3 * half, outputs))


def body(video, w_spatial, norm_gain, norm_shift, w_time):
    count, height, width, channels = video.shape
    assert count == 1 and lax.axis_size("fsdp") == 2
    pixels = height * width
    side = lax.axis_index("fsdp")
    blocks = lax.axis_size("video") * 2
    position = lax.axis_index("video") * 2 + side

    route = []
    for j in range(blocks):
        target = j + 1 if j % 2 == 1 else j - 1
        if 0 <= target < blocks and min(j, target) % CLIP != CLIP - 1:
            route.append((j, target))
    frame = video.reshape(pixels, channels)
    edge_video = lax.ppermute(frame, ("video", "fsdp"), route)
    other_spatial = swap_pair(w_spatial)
    other_time = swap_pair(w_time)

    gain = norm_gain.reshape(1, channels)
    shift = norm_shift.reshape(1, channels)
    sides = side.reshape(1).astype(jnp.int32)
    hidden = conv_norm(frame, w_spatial, other_spatial, gain, shift, sides, width)
    partner = swap_pair(hidden)
    keep_prev = (position % CLIP != 0).astype(jnp.int32)
    keep_next = (position % CLIP != CLIP - 1).astype(jnp.int32)
    keep_edge = jnp.where(side == 0, keep_prev, keep_next)
    keep_partner = jnp.where(side == 0, keep_next, keep_prev)
    scalars = jnp.stack([side.astype(jnp.int32), keep_edge, keep_partner])
    result = edge_temporal(edge_video, w_spatial, other_spatial, gain, shift, hidden, partner,
                           w_time, other_time, scalars, width)
    return result.reshape(count, height, width, channels)


def solution(mesh):
    placed = (
        P(("groups", "video", "fsdp"), None, None, None),
        P(None, None, "fsdp", None),
        P(),
        P(),
        P(None, "fsdp", None),
    )
    return jax.shard_map(
        body,
        mesh=mesh,
        in_specs=placed,
        out_specs=P(("groups", "video", "fsdp"), None, None, None),
        check_vma=False,
    )
```

```python
import functools

import jax
import jax.numpy as jnp
from jax import lax
from jax.experimental import pallas as pl
from jax.experimental.pallas import tpu as pltpu
from jax.sharding import PartitionSpec as P

GROUPS = 32
CLIP = 16
EPS = 1e-05


def swap_pair(block):
    return lax.ppermute(block, "fsdp", [(0, 1), (1, 0)])


def group_sum(row, size):
    lanes = lax.broadcasted_iota(jnp.int32, row.shape, 1)
    width = row.shape[1]
    step = 1
    while step < size:
        up = pltpu.roll(row, width - step, 1)
        down = pltpu.roll(row, step, 1)
        row = row + jnp.where((lanes & step) == 0, up, down)
        step *= 2
    return row


def build_lhs(halves, lhs_ref, width):
    rows, half = halves[0][1].shape
    col = lax.broadcasted_iota(jnp.int32, (rows, half), 0) % width
    zeros = jnp.zeros((width, half), jnp.bfloat16)
    for h, x in halves:
        xf = x.astype(jnp.float32)
        left = jnp.where(col == 0, 0.0, pltpu.roll(xf, 1, 0)).astype(jnp.bfloat16)
        right = jnp.where(col == width - 1, 0.0, pltpu.roll(xf, rows - 1, 0)).astype(jnp.bfloat16)
        for dx, v in enumerate((left, xf.astype(jnp.bfloat16), right)):
            for dy in range(3):
                lo = (dy * 3 + dx) * half
                cols = slice(lo, lo + half)
                if dy == 0:
                    lhs_ref[h, :width, cols] = zeros
                    lhs_ref[h, width:, cols] = v[: rows - width]
                elif dy == 1:
                    lhs_ref[h, :, cols] = v
                else:
                    lhs_ref[h, : rows - width, cols] = v[width:]
                    lhs_ref[h, rows - width :, cols] = zeros


def own_conv_kernel(side_ref, xa_ref, xb_ref, wa_ref, wb_ref, gain_ref, shift_ref, later_hbm,
                    o_ref, lhs_ref, *, width, group):
    conv_norm_kernel(side_ref, xa_ref, xb_ref, wa_ref, wb_ref, gain_ref, shift_ref, o_ref,
                     lhs_ref, width=width, group=group)


def conv_norm_kernel(side_ref, xa_ref, xb_ref, wa_ref, wb_ref, gain_ref, shift_ref, o_ref,
                     lhs_ref, *, width, group):
    build_lhs(((0, xa_ref[...]), (1, xb_ref[...])), lhs_ref, width)
    dots_norm(lhs_ref, wa_ref, wb_ref, gain_ref, shift_ref, o_ref, group)


def dots_norm(lhs_ref, wa_ref, wb_ref, gain_ref, shift_ref, o_ref, group):
    rows = lhs_ref.shape[1]
    acc = jnp.dot(lhs_ref[0], wa_ref[...], preferred_element_type=jnp.float32) + jnp.dot(
        lhs_ref[1], wb_ref[...], preferred_element_type=jnp.float32
    )
    count = rows * group
    total = jnp.broadcast_to(jnp.sum(acc, axis=0, keepdims=True), (8, acc.shape[1]))
    mean = group_sum(total, group)[0:1] / count
    d = acc - mean
    spread = jnp.broadcast_to(jnp.sum(d * d, axis=0, keepdims=True), (8, acc.shape[1]))
    variance = group_sum(spread, group)[0:1] / count
    v = d * lax.rsqrt(variance + EPS) * gain_ref[...] + shift_ref[...]
    o_ref[...] = (v / (1.0 + jnp.exp(-v))).astype(o_ref.dtype)


def conv_norm(frame, w_mine, w_other, gain, shift, side, width, later, split=1):
    rows, channels = frame.shape
    half = w_mine.shape[2]
    outputs = w_mine.shape[3]
    group = outputs // GROUPS
    block = outputs // split
    kernel = functools.partial(own_conv_kernel, width=width, group=group)
    weight_block = pl.BlockSpec((9 * half, block), lambda n, s: (0, n))
    row_block = pl.BlockSpec((1, block), lambda n, s: (0, n))
    return pl.pallas_call(
        kernel,
        out_shape=jax.ShapeDtypeStruct((rows, outputs), jnp.bfloat16),
        grid_spec=pltpu.PrefetchScalarGridSpec(
            num_scalar_prefetch=1,
            grid=(split,),
            in_specs=[
                pl.BlockSpec((rows, half), lambda n, s: (0, s[0])),
                pl.BlockSpec((rows, half), lambda n, s: (0, 1 - s[0])),
                weight_block,
                weight_block,
                row_block,
                row_block,
                pl.BlockSpec(memory_space=pl.ANY),
            ],
            out_specs=pl.BlockSpec((rows, block), lambda n, s: (0, n)),
            scratch_shapes=[pltpu.VMEM((2, rows, 9 * half), jnp.bfloat16)],
        ),
        compiler_params=pltpu.CompilerParams(dimension_semantics=("arbitrary",)),
    )(side, frame, frame, w_mine.reshape(9 * half, outputs), w_other.reshape(9 * half, outputs),
      gain, shift, later)


def edge_temporal_kernel(s_ref, x_ref, wa_ref, wb_ref, gain_ref, shift_ref,
                         cur_hbm, partner_hbm, wtm_hbm, wto_hbm, o_ref,
                         lhs_ref, edge_v, cur_v, partner_v, wtm_v, wto_v, tl_ref, sem,
                         *, width, group):
    copies = [
        pltpu.make_async_copy(src, dst, sem.at[i])
        for i, (src, dst) in enumerate(
            ((cur_hbm, cur_v), (partner_hbm, partner_v), (wtm_hbm, wtm_v), (wto_hbm, wto_v))
        )
    ]
    for copy in copies:
        copy.start()
    half = x_ref.shape[1] // 2
    for side in range(2):
        @pl.when(s_ref[0] == side)
        def _prepare():
            build_lhs(
                [((h + side) % 2, x_ref[:, h * half : (h + 1) * half]) for h in range(2)],
                lhs_ref, width,
            )
    dots_norm(lhs_ref, wa_ref, wb_ref, gain_ref, shift_ref, edge_v, group)
    for copy in copies:
        copy.wait()

    rows = x_ref.shape[0]
    keep_edge = s_ref[1] != 0
    keep_partner = s_ref[2] != 0
    for side in range(2):
        @pl.when(s_ref[0] == side)
        def _fill():
            mine = slice(side * half, (side + 1) * half)
            other = slice((1 - side) * half, (2 - side) * half)
            for h, cols in enumerate((mine, other)):
                e = edge_v[:, cols]
                p = partner_v[:, cols]
                e = jnp.where(keep_edge, e, jnp.zeros_like(e))
                p = jnp.where(keep_partner, p, jnp.zeros_like(p))
                before, after = (e, p) if side == 0 else (p, e)
                tl_ref[h, :, :half] = before
                tl_ref[h, :, half : 2 * half] = cur_v[:, cols]
                tl_ref[h, :, 2 * half :] = after

    f32 = jnp.float32
    total = jnp.dot(tl_ref[0], wtm_v[...], preferred_element_type=f32) + jnp.dot(
        tl_ref[1], wto_v[...], preferred_element_type=f32
    )
    o_ref[...] = (cur_v[...].astype(f32) + total).astype(o_ref.dtype)


def edge_temporal(frame, w_mine, w_other, gain, shift, cur, partner, t_mine, t_other, scalars,
                  width):
    rows, channels = frame.shape
    half = w_mine.shape[2]
    outputs = w_mine.shape[3]
    group = outputs // GROUPS
    kernel = functools.partial(edge_temporal_kernel, width=width, group=group)
    weight_block = pl.BlockSpec((9 * half, outputs), lambda n, s: (0, 0))
    row_block = pl.BlockSpec((1, outputs), lambda n, s: (0, 0))
    anywhere = pl.BlockSpec(memory_space=pl.ANY)
    in_vmem = pl.BlockSpec(memory_space=pltpu.VMEM)
    return pl.pallas_call(
        kernel,
        out_shape=jax.ShapeDtypeStruct((rows, outputs), jnp.bfloat16),
        grid_spec=pltpu.PrefetchScalarGridSpec(
            num_scalar_prefetch=1,
            grid=(1,),
            in_specs=[
                in_vmem,
                weight_block,
                weight_block,
                row_block,
                row_block,
                anywhere,
                anywhere,
                anywhere,
                anywhere,
            ],
            out_specs=pl.BlockSpec((rows, outputs), lambda n, s: (0, 0)),
            scratch_shapes=[
                pltpu.VMEM((2, rows, 9 * half), jnp.bfloat16),
                pltpu.VMEM((rows, outputs), jnp.bfloat16),
                pltpu.VMEM((rows, channels), jnp.bfloat16),
                pltpu.VMEM((rows, channels), jnp.bfloat16),
                pltpu.VMEM((3 * half, outputs), jnp.bfloat16),
                pltpu.VMEM((3 * half, outputs), jnp.bfloat16),
                pltpu.VMEM((2, rows, 3 * half), jnp.bfloat16),
                pltpu.SemaphoreType.DMA((4,)),
            ],
        ),
        compiler_params=pltpu.CompilerParams(dimension_semantics=("arbitrary",)),
    )(scalars, frame, w_mine.reshape(9 * half, outputs), w_other.reshape(9 * half, outputs),
      gain, shift, cur, partner, t_mine.reshape(3 * half, outputs),
      t_other.reshape(3 * half, outputs))


def body(video, w_spatial, norm_gain, norm_shift, w_time):
    count, height, width, channels = video.shape
    assert count == 1 and lax.axis_size("fsdp") == 2
    pixels = height * width
    side = lax.axis_index("fsdp")
    blocks = lax.axis_size("video") * 2
    position = lax.axis_index("video") * 2 + side

    route = []
    for j in range(blocks):
        target = j + 1 if j % 2 == 1 else j - 1
        if 0 <= target < blocks and min(j, target) % CLIP != CLIP - 1:
            route.append((j, target))
    frame = video.reshape(pixels, channels)
    edge_video = lax.ppermute(frame, ("video", "fsdp"), route)
    other_spatial = swap_pair(w_spatial)
    other_time = swap_pair(w_time)

    gain = norm_gain.reshape(1, channels)
    shift = norm_shift.reshape(1, channels)
    sides = side.reshape(1).astype(jnp.int32)
    hidden = conv_norm(frame, w_spatial, other_spatial, gain, shift, sides, width, other_time)
    partner = swap_pair(hidden)
    keep_prev = (position % CLIP != 0).astype(jnp.int32)
    keep_next = (position % CLIP != CLIP - 1).astype(jnp.int32)
    keep_edge = jnp.where(side == 0, keep_prev, keep_next)
    keep_partner = jnp.where(side == 0, keep_next, keep_prev)
    scalars = jnp.stack([side.astype(jnp.int32), keep_edge, keep_partner])
    result = edge_temporal(edge_video, w_spatial, other_spatial, gain, shift, hidden, partner,
                           w_time, other_time, scalars, width)
    return result.reshape(count, height, width, channels)


def solution(mesh):
    placed = (
        P(("groups", "video", "fsdp"), None, None, None),
        P(None, None, "fsdp", None),
        P(),
        P(),
        P(None, "fsdp", None),
    )
    return jax.shard_map(
        body,
        mesh=mesh,
        in_specs=placed,
        out_specs=P(("groups", "video", "fsdp"), None, None, None),
        check_vma=False,
    )
```

```python
import functools

import jax
import jax.numpy as jnp
from jax import lax
from jax.experimental import pallas as pl
from jax.experimental.pallas import tpu as pltpu
from jax.sharding import PartitionSpec as P

GROUPS = 32
CLIP = 16
EPS = 1e-05


def swap_pair(block):
    return lax.ppermute(block, "fsdp", [(0, 1), (1, 0)])


def group_sum(row, size):
    lanes = lax.broadcasted_iota(jnp.int32, row.shape, 1)
    width = row.shape[1]
    step = 1
    while step < size:
        up = pltpu.roll(row, width - step, 1)
        down = pltpu.roll(row, step, 1)
        row = row + jnp.where((lanes & step) == 0, up, down)
        step *= 2
    return row


def conv_norm_kernel(side_ref, xa_ref, xb_ref, wa_ref, wb_ref, gain_ref, shift_ref, o_ref,
                     lhs_ref, *, width, group):
    rows, half = xa_ref.shape

    @pl.when(pl.program_id(0) == 0)
    def _prepare():
        col = lax.broadcasted_iota(jnp.int32, (rows, half), 0) % width
        zeros = jnp.zeros((width, half), jnp.bfloat16)
        for h, x_ref in enumerate((xa_ref, xb_ref)):
            xf = x_ref[...].astype(jnp.float32)
            left = jnp.where(col == 0, 0.0, pltpu.roll(xf, 1, 0)).astype(jnp.bfloat16)
            right = jnp.where(col == width - 1, 0.0, pltpu.roll(xf, rows - 1, 0)).astype(jnp.bfloat16)
            for dx, v in enumerate((left, xf.astype(jnp.bfloat16), right)):
                for dy in range(3):
                    lo = (dy * 3 + dx) * half
                    cols = slice(lo, lo + half)
                    if dy == 0:
                        lhs_ref[h, :width, cols] = zeros
                        lhs_ref[h, width:, cols] = v[: rows - width]
                    elif dy == 1:
                        lhs_ref[h, :, cols] = v
                    else:
                        lhs_ref[h, : rows - width, cols] = v[width:]
                        lhs_ref[h, rows - width :, cols] = zeros

    acc = jnp.dot(lhs_ref[0], wa_ref[...], preferred_element_type=jnp.float32) + jnp.dot(
        lhs_ref[1], wb_ref[...], preferred_element_type=jnp.float32
    )
    count = rows * group
    total = jnp.broadcast_to(jnp.sum(acc, axis=0, keepdims=True), (8, acc.shape[1]))
    mean = group_sum(total, group)[0:1] / count
    d = acc - mean
    spread = jnp.broadcast_to(jnp.sum(d * d, axis=0, keepdims=True), (8, acc.shape[1]))
    variance = group_sum(spread, group)[0:1] / count
    v = d * lax.rsqrt(variance + EPS) * gain_ref[...] + shift_ref[...]
    hidden = (v / (1.0 + jnp.exp(-v))).astype(jnp.bfloat16)
    if o_ref is None:
        return hidden
    o_ref[...] = hidden.astype(o_ref.dtype)


def conv_norm(frame, w_mine, w_other, gain, shift, side, width, split=1):
    rows, channels = frame.shape
    half = w_mine.shape[2]
    outputs = w_mine.shape[3]
    group = outputs // GROUPS
    block = outputs // split
    kernel = functools.partial(conv_norm_kernel, width=width, group=group)
    weight_block = pl.BlockSpec((9 * half, block), lambda n, s: (0, n))
    row_block = pl.BlockSpec((1, block), lambda n, s: (0, n))
    return pl.pallas_call(
        kernel,
        out_shape=jax.ShapeDtypeStruct((rows, outputs), jnp.bfloat16),
        grid_spec=pltpu.PrefetchScalarGridSpec(
            num_scalar_prefetch=1,
            grid=(split,),
            in_specs=[
                pl.BlockSpec((rows, half), lambda n, s: (0, s[0])),
                pl.BlockSpec((rows, half), lambda n, s: (0, 1 - s[0])),
                weight_block,
                weight_block,
                row_block,
                row_block,
            ],
            out_specs=pl.BlockSpec((rows, block), lambda n, s: (0, n)),
            scratch_shapes=[pltpu.VMEM((2, rows, 9 * half), jnp.bfloat16)],
        ),
        compiler_params=pltpu.CompilerParams(dimension_semantics=("arbitrary",)),
    )(side, frame, frame, w_mine.reshape(9 * half, outputs), w_other.reshape(9 * half, outputs),
      gain, shift)


def edge_temporal_kernel(s_ref, xa_ref, xb_ref, wa_ref, wb_ref, gain_ref, shift_ref,
                         cur_hbm, partner_hbm, wtm_hbm, wto_hbm, o_ref,
                         lhs_ref, cur_v, partner_v, wtm_v, wto_v, tl_ref, sem,
                         *, width, group):
    copies = [
        pltpu.make_async_copy(src, dst, sem.at[i])
        for i, (src, dst) in enumerate(
            ((cur_hbm, cur_v), (partner_hbm, partner_v), (wtm_hbm, wtm_v), (wto_hbm, wto_v))
        )
    ]
    for copy in copies:
        copy.start()
    edge_h = conv_norm_kernel(s_ref, xa_ref, xb_ref, wa_ref, wb_ref, gain_ref, shift_ref, None,
                              lhs_ref, width=width, group=group)
    rows, half = xa_ref.shape
    keep_edge = s_ref[1] != 0
    keep_partner = s_ref[2] != 0
    edge_h = jnp.where(keep_edge, edge_h, jnp.zeros_like(edge_h))
    for side in range(2):
        @pl.when(s_ref[0] == side)
        def _edge():
            mine = slice(side * half, (side + 1) * half)
            other = slice((1 - side) * half, (2 - side) * half)
            at = slice(0, half) if side == 0 else slice(2 * half, 3 * half)
            for h, cols in enumerate((mine, other)):
                tl_ref[h, :, at] = edge_h[:, cols]
    for copy in copies:
        copy.wait()

    for side in range(2):
        @pl.when(s_ref[0] == side)
        def _fill():
            mine = slice(side * half, (side + 1) * half)
            other = slice((1 - side) * half, (2 - side) * half)
            at = slice(2 * half, 3 * half) if side == 0 else slice(0, half)
            for h, cols in enumerate((mine, other)):
                p = partner_v[:, cols]
                tl_ref[h, :, at] = jnp.where(keep_partner, p, jnp.zeros_like(p))
                tl_ref[h, :, half : 2 * half] = cur_v[:, cols]

    f32 = jnp.float32
    total = jnp.dot(tl_ref[0], wtm_v[...], preferred_element_type=f32) + jnp.dot(
        tl_ref[1], wto_v[...], preferred_element_type=f32
    )
    o_ref[...] = (cur_v[...].astype(f32) + total).astype(o_ref.dtype)


def edge_temporal(frame, w_mine, w_other, gain, shift, cur, partner, t_mine, t_other, scalars,
                  width):
    rows, channels = frame.shape
    half = w_mine.shape[2]
    outputs = w_mine.shape[3]
    group = outputs // GROUPS
    kernel = functools.partial(edge_temporal_kernel, width=width, group=group)
    weight_block = pl.BlockSpec((9 * half, outputs), lambda n, s: (0, 0))
    row_block = pl.BlockSpec((1, outputs), lambda n, s: (0, 0))
    anywhere = pl.BlockSpec(memory_space=pl.ANY)
    return pl.pallas_call(
        kernel,
        out_shape=jax.ShapeDtypeStruct((rows, outputs), jnp.bfloat16),
        grid_spec=pltpu.PrefetchScalarGridSpec(
            num_scalar_prefetch=1,
            grid=(1,),
            in_specs=[
                pl.BlockSpec((rows, half), lambda n, s: (0, s[0])),
                pl.BlockSpec((rows, half), lambda n, s: (0, 1 - s[0])),
                weight_block,
                weight_block,
                row_block,
                row_block,
                anywhere,
                anywhere,
                anywhere,
                anywhere,
            ],
            out_specs=pl.BlockSpec((rows, outputs), lambda n, s: (0, 0)),
            scratch_shapes=[
                pltpu.VMEM((2, rows, 9 * half), jnp.bfloat16),
                pltpu.VMEM((rows, channels), jnp.bfloat16),
                pltpu.VMEM((rows, channels), jnp.bfloat16),
                pltpu.VMEM((3 * half, outputs), jnp.bfloat16),
                pltpu.VMEM((3 * half, outputs), jnp.bfloat16),
                pltpu.VMEM((2, rows, 3 * half), jnp.bfloat16),
                pltpu.SemaphoreType.DMA((4,)),
            ],
        ),
        compiler_params=pltpu.CompilerParams(dimension_semantics=("arbitrary",)),
    )(scalars, frame, frame, w_mine.reshape(9 * half, outputs), w_other.reshape(9 * half, outputs),
      gain, shift, cur, partner, t_mine.reshape(3 * half, outputs),
      t_other.reshape(3 * half, outputs))


def body(video, w_spatial, norm_gain, norm_shift, w_time):
    count, height, width, channels = video.shape
    assert count == 1 and lax.axis_size("fsdp") == 2
    pixels = height * width
    side = lax.axis_index("fsdp")
    blocks = lax.axis_size("video") * 2
    position = lax.axis_index("video") * 2 + side

    route = []
    for j in range(blocks):
        target = j + 1 if j % 2 == 1 else j - 1
        if 0 <= target < blocks and min(j, target) % CLIP != CLIP - 1:
            route.append((j, target))
    frame = video.reshape(pixels, channels)
    edge_video = lax.ppermute(frame, ("video", "fsdp"), route)
    other_spatial = swap_pair(w_spatial)
    other_time = swap_pair(w_time)

    gain = norm_gain.reshape(1, channels)
    shift = norm_shift.reshape(1, channels)
    sides = side.reshape(1).astype(jnp.int32)
    hidden = conv_norm(frame, w_spatial, other_spatial, gain, shift, sides, width)
    partner = swap_pair(hidden)
    keep_prev = (position % CLIP != 0).astype(jnp.int32)
    keep_next = (position % CLIP != CLIP - 1).astype(jnp.int32)
    keep_edge = jnp.where(side == 0, keep_prev, keep_next)
    keep_partner = jnp.where(side == 0, keep_next, keep_prev)
    scalars = jnp.stack([side.astype(jnp.int32), keep_edge, keep_partner])
    result = edge_temporal(edge_video, w_spatial, other_spatial, gain, shift, hidden, partner,
                           w_time, other_time, scalars, width)
    return result.reshape(count, height, width, channels)


def solution(mesh):
    placed = (
        P(("groups", "video", "fsdp"), None, None, None),
        P(None, None, "fsdp", None),
        P(),
        P(),
        P(None, "fsdp", None),
    )
    return jax.shard_map(
        body,
        mesh=mesh,
        in_specs=placed,
        out_specs=P(("groups", "video", "fsdp"), None, None, None),
        check_vma=False,
    )
```
